256 devices in a mesh: wave: 8 (over z_lo, core), tile: 32 (over x, z_hi, y).
Axes of the slice: x: 4, y: 4, z: 8 (z_hi: 2, z_lo: 4; z = z_hi * 4 + z_lo), core: 2. Of those that a mesh axis runs over, the one named last changes fastest.
Arguments:
- thickness: float32 [32, 256, 256], P('tile'), may hold values from 0 to 1
- illumination: float32 [16, 2, 256, 256], P('wave'), may hold values from -6 to 6
- absorb: float32 [16], P('wave'), may hold values from 0.1 to 0.8
- phases: float32 [16], P('wave'), may hold values from 0.1 to 0.8
- amplitudes: bfloat16 [32, 6, 16, 256, 256], P('tile', None, 'wave'), may hold values from 0.049804688 to 0.5
- positions: int32 [32, 6, 2], P('tile'), may hold values from 0 to 255, as said below
- batch_order: int32 [32, 6], P('tile'), may hold values from 0 to 5, each once within a row
- live_slots: int32 [32, 3, 2], P('tile'), may hold values from 0 to 1, as said below
Outputs:
- thickness_new: float32 [32, 256, 256], P('tile')
The draws below stay inside these ranges and needn't reach their ends.
Inputs may be any that keep to these rules, and one draw needn't show every extreme that they name: `positions`: offsets inside the tile that owns the pattern; the 256 x 256 window from every slot's corner lies inside the object. `live_slots`: in every batch at least one tile has its slot 0 live.
All inputs are finite; a program needn't handle non-finite values.
Results may differ from the reference program's by a relative error of at most 0.0003.
Values sent between devices are 32-bit elements; how exact they have to be, the bound alone decides.
No kernel may reach another device: no remote copies, remote signals or barrier semaphores. Data moves between devices by JAX's collectives and lax.ppermute only.
A program may use at most 64 MiB of HBM per device.

```python
import math
import jax
import jax.numpy as jnp
from jax import lax

WIN = 256
WAVES = 16
GRID_X = 8
TH = 256
TW = 256
SLOTS = 2
BATCHES = 3
OUTER = 1
SCANS = 6
TILES = 32
NR = 1024
NC = 2048


def draw_positions(key, part):
    key_rows = jax.random.fold_in(key, 11)
    key_cols = jax.random.fold_in(key, 12)
    tile_ids = jnp.arange(TILES, dtype=jnp.int32)
    tile_rows = TILES // GRID_X
    row_limit = jnp.where(tile_ids // GRID_X == tile_rows - 1, TH - WIN + 1, TH).astype(jnp.int32)
    col_limit = jnp.where(tile_ids % GRID_X == GRID_X - 1, TW - WIN + 1, TW).astype(jnp.int32)
    rows_drawn = jax.random.randint(key_rows, (TILES, SCANS), 0, row_limit[:, None])
    cols_drawn = jax.random.randint(key_cols, (TILES, SCANS), 0, col_limit[:, None])
    rows_drawn = rows_drawn.at[0, 0].set(TH - 1).at[0, 1].set(0)
    cols_drawn = cols_drawn.at[0, 0].set(TW - 1).at[0, 1].set(0)
    return jnp.stack([rows_drawn, cols_drawn], -1).astype(jnp.int32)


def draw_live_slots(key, part):
    key_one = jax.random.fold_in(key, 21)
    key_two = jax.random.fold_in(key, 22)
    drawn = jax.random.randint(key_one, (TILES, BATCHES, SLOTS), 0, 10) < 7
    chosen = jax.random.randint(key_two, (BATCHES,), 0, TILES)
    tile_ids = jnp.arange(TILES, dtype=jnp.int32)[:, None, None]
    slot_ids = jnp.arange(SLOTS, dtype=jnp.int32)[None, None, :]
    forced = (tile_ids == chosen[None, :, None]) & (slot_ids == 0)
    return (drawn | forced).astype(jnp.int32)


def block_scale(key, extent, cuts, smallest, high):
    level, own = 1.0, jax.random.fold_in(key, 6)
    for position, parts in cuts:
        steps = jnp.exp(jax.random.uniform(jax.random.fold_in(own, position), (parts,), jnp.float32, smallest / len(cuts), high / len(cuts)))
        level = level * jnp.repeat(steps, extent[position] // parts).reshape([-1 if axis == position else 1 for axis in range(len(extent))])
    return level


def bell_draw(key, dims, deviation, bound, pieces=(), kind=jnp.bfloat16):
    values = jax.random.normal(key, dims, jnp.float32) * deviation
    if len(pieces) > 0:
        values = block_scale(key, dims, pieces, -0.22, 0.18) * values
    return jnp.clip(values, min=-bound, max=bound).astype(kind)


def setup_inputs(seed: int = 0) -> dict:
    key_list = jax.random.split(jax.random.key(seed), 9)
    thickness = jnp.clip(1.0 * jax.random.uniform(key_list[0], (TILES, TH, TW), jnp.float32) ** block_scale(key_list[0], (TILES, TH, TW), ((0, 32),), -0.2, 0.2), 0.0, 1.0)
    illumination = bell_draw(key_list[1], (WAVES, 2, WIN, WIN), 1.0, 6.0, ((0, 8),), jnp.float32)
    absorb = jnp.clip(jnp.exp(math.log(0.8) - 2.0794415 * jax.random.uniform(key_list[2], (WAVES,), jnp.float32) ** block_scale(key_list[2], (WAVES,), ((0, 8),), -0.2, 0.2)), 0.1, 0.8)
    phases = jnp.clip(jnp.exp(math.log(0.8) - 2.0794415 * jax.random.uniform(key_list[3], (WAVES,), jnp.float32) ** block_scale(key_list[3], (WAVES,), ((0, 8),), -0.2, 0.2)), 0.1, 0.8)
    amplitudes = jnp.clip(jnp.exp(math.log(0.5) - 2.306499 * jax.random.uniform(key_list[4], (TILES, SCANS, WAVES, WIN, WIN), jnp.float32) ** block_scale(key_list[4], (TILES, SCANS, WAVES, WIN, WIN), ((0, 32), (2, 8)), -0.2, 0.2)), 0.049804688, 0.5).astype(jnp.bfloat16)
    positions = draw_positions(jax.random.fold_in(key_list[8], 71), 0)
    batch_order = jax.vmap(lambda own: jax.random.permutation(own, SCANS))(jax.random.split(key_list[6], TILES)).reshape((TILES, SCANS)).astype(jnp.int32)
    live_slots = draw_live_slots(jax.random.fold_in(key_list[8], 71), 0)
    return {"thickness": thickness, "illumination": illumination, "absorb": absorb, "phases": phases, "amplitudes": amplitudes, "positions": positions, "batch_order": batch_order, "live_slots": live_slots}


def tables(points):
    counter = jnp.arange(points, dtype=jnp.int32)
    angles = 2.0 * math.pi / points * (counter[:, None] * counter[None, :] % points).astype(jnp.float32)
    factor = 1.0 / math.sqrt(points)
    return ((jnp.cos(angles) * factor).astype(jnp.bfloat16), (-jnp.sin(angles) * factor).astype(jnp.bfloat16))

def left_apply(real_part, imag_part, left_real, left_imag):
    points = real_part.shape[0]
    stacked = jnp.concatenate([real_part, imag_part], 0).astype(jnp.float32)
    joined = jnp.concatenate([left_real, left_imag], -1).astype(jnp.float32)
    product = jnp.einsum('ij,...jk->...ik', stacked, joined)
    return (product[..., :points, :points] - product[..., points:, points:], product[..., :points, points:] + product[..., points:, :points])

def right_apply(real_part, imag_part, left_real, left_imag):
    points = real_part.shape[0]
    stacked = jnp.concatenate([real_part, imag_part], 1).astype(jnp.float32)
    joined = jnp.concatenate([left_real, left_imag], -2).astype(jnp.float32)
    product = jnp.einsum('...ij,jk->...ik', joined, stacked)
    return (product[..., :points, :points] - product[..., points:, points:], product[..., :points, points:] + product[..., points:, :points])

def window_terms(cells, illumination, absorb, phases, measured, alive, cos_table, sin_table):
    absorb_col = absorb[None, :, None, None]
    phase_col = phases[None, :, None, None]
    spread = cells[:, None, :, :]
    magnitude = jnp.exp(-absorb_col * spread)
    object_real = magnitude * jnp.cos(phase_col * spread)
    object_imag = magnitude * jnp.sin(phase_col * spread)
    probe_real = illumination[None, :, 0]
    probe_imag = illumination[None, :, 1]
    wave_real = probe_real * object_real - probe_imag * object_imag
    wave_imag = probe_real * object_imag + probe_imag * object_real
    half_real, half_imag = left_apply(cos_table, sin_table, wave_real.astype(jnp.bfloat16), wave_imag.astype(jnp.bfloat16))
    far_real, far_imag = right_apply(cos_table, sin_table, half_real.astype(jnp.bfloat16), half_imag.astype(jnp.bfloat16))
    modulus = jnp.sqrt(far_real * far_real + far_imag * far_imag + 0.25)
    ratio = measured.astype(jnp.float32) / modulus
    fixed_real = (far_real * ratio).astype(jnp.bfloat16)
    fixed_imag = (far_imag * ratio).astype(jnp.bfloat16)
    back_real, back_imag = left_apply(cos_table, -sin_table, fixed_real, fixed_imag)
    new_real, new_imag = right_apply(cos_table, -sin_table, back_real.astype(jnp.bfloat16), back_imag.astype(jnp.bfloat16))
    slope_real = -absorb_col * wave_real - phase_col * wave_imag
    slope_imag = -absorb_col * wave_imag + phase_col * wave_real
    change_real = new_real - wave_real
    change_imag = new_imag - wave_imag
    weight_live = alive.astype(jnp.float32)[:, None, None]
    numerator = lax.optimization_barrier(jnp.sum(slope_real * change_real + slope_imag * change_imag, axis=1)) * weight_live
    weights = lax.optimization_barrier(jnp.sum(slope_real * slope_real + slope_imag * slope_imag, axis=1)) * weight_live
    return (numerator, weights)

def reference(thickness, illumination, absorb, phases, amplitudes, positions, batch_order, live_slots):
    tile_rows = TILES // GRID_X
    object_map = thickness.reshape(tile_rows, GRID_X, TH, TW).transpose(0, 2, 1, 3).reshape(NR, NC)
    tile_ids = jnp.arange(TILES, dtype=jnp.int32)
    row_base = tile_ids // GRID_X * TH
    col_base = tile_ids % GRID_X * TW
    cos_table, sin_table = tables(WIN)
    for iteration in range(OUTER):
        for batch_index in range(BATCHES):
            chosen = batch_order[:, batch_index * SLOTS:(batch_index + 1) * SLOTS]
            places = jax.vmap(lambda table, picked: table[picked])(positions, chosen)
            measured = jax.vmap(lambda table, picked: table[picked])(amplitudes, chosen)
            global_rows = (places[:, :, 0] + row_base[:, None]).astype(jnp.int32)
            global_cols = (places[:, :, 1] + col_base[:, None]).astype(jnp.int32)
            alive = live_slots[:, batch_index, :]
            current = object_map

            def one_tile(inputs):
                rows_here, cols_here, measured_here, alive_here = inputs
                cells = jax.vmap(lambda row_at, col_at: lax.dynamic_slice(current, (row_at, col_at), (WIN, WIN)))(rows_here, cols_here)
                return window_terms(cells, illumination, absorb, phases, measured_here, alive_here, cos_table, sin_table)
            numer_win, weight_win = lax.map(one_tile, (global_rows, global_cols, measured, alive))
            numer_flat = numer_win.reshape(TILES * SLOTS, WIN, WIN)
            weight_flat = weight_win.reshape(TILES * SLOTS, WIN, WIN)
            rows_flat = global_rows.reshape(TILES * SLOTS)
            cols_flat = global_cols.reshape(TILES * SLOTS)

            def add_window(slot_index, totals):
                numer_map, weight_map = totals
                row_at = rows_flat[slot_index]
                col_at = cols_flat[slot_index]
                numer_map = lax.dynamic_update_slice(numer_map, lax.dynamic_slice(numer_map, (row_at, col_at), (WIN, WIN)) + numer_flat[slot_index], (row_at, col_at))
                weight_map = lax.dynamic_update_slice(weight_map, lax.dynamic_slice(weight_map, (row_at, col_at), (WIN, WIN)) + weight_flat[slot_index], (row_at, col_at))
                return (numer_map, weight_map)
            empty = jnp.zeros((NR, NC), jnp.float32)
            numer_map, weight_map = lax.fori_loop(0, TILES * SLOTS, add_window, (empty, empty))
            largest = jnp.max(weight_map)
            object_map = object_map + 0.5 * numer_map / (0.75 * weight_map + 0.25 * largest)
    return object_map.reshape(tile_rows, TH, GRID_X, TW).transpose(0, 2, 1, 3).reshape(TILES, TH, TW)
```

```python
import math

import jax
import jax.numpy as jnp
from jax import lax
from jax.sharding import PartitionSpec as P

GRID_X = 8
BATCHES = 3


def passed_along(block, axis, distance):
    devices = range(lax.axis_size(axis))
    route = [(i - distance, i) for i in devices if i - distance in devices]
    return lax.ppermute(block, axis, route)


def tables(points):
    counter = jnp.arange(points, dtype=jnp.int32)
    angles = (
        2.0 * math.pi / points * (counter[:, None] * counter[None, :] % points).astype(jnp.float32)
    )
    factor = 1.0 / math.sqrt(points)
    return (
        (jnp.cos(angles) * factor).astype(jnp.bfloat16),
        (-jnp.sin(angles) * factor).astype(jnp.bfloat16),
    )


def left_apply(real_part, imag_part, left_real, left_imag):
    points = real_part.shape[0]
    stacked = jnp.concatenate([real_part, imag_part], 0)
    joined = jnp.concatenate([left_real, left_imag], -1)
    product = jnp.einsum("ij,...jk->...ik", stacked, joined, preferred_element_type=jnp.float32)
    return (
        product[..., :points, :points] - product[..., points:, points:],
        product[..., :points, points:] + product[..., points:, :points],
    )


def right_apply(real_part, imag_part, left_real, left_imag):
    points = real_part.shape[0]
    stacked = jnp.concatenate([real_part, imag_part], 1)
    joined = jnp.concatenate([left_real, left_imag], -2)
    product = jnp.einsum("...ij,jk->...ik", joined, stacked, preferred_element_type=jnp.float32)
    return (
        product[..., :points, :points] - product[..., points:, points:],
        product[..., :points, points:] + product[..., points:, :points],
    )


def window_terms(cells, illumination, absorb, phases, measured, alive, cos_table, sin_table):
    absorb_col = absorb[None, :, None, None]
    phase_col = phases[None, :, None, None]
    spread = cells[:, None, :, :]
    magnitude = jnp.exp(-absorb_col * spread)
    object_real = magnitude * jnp.cos(phase_col * spread)
    object_imag = magnitude * jnp.sin(phase_col * spread)
    probe_real = illumination[None, :, 0]
    probe_imag = illumination[None, :, 1]
    wave_real = probe_real * object_real - probe_imag * object_imag
    wave_imag = probe_real * object_imag + probe_imag * object_real
    half_real, half_imag = left_apply(
        cos_table, sin_table, wave_real.astype(jnp.bfloat16), wave_imag.astype(jnp.bfloat16)
    )
    far_real, far_imag = right_apply(
        cos_table, sin_table, half_real.astype(jnp.bfloat16), half_imag.astype(jnp.bfloat16)
    )
    modulus = jnp.sqrt(far_real * far_real + far_imag * far_imag + 0.25)
    ratio = measured.astype(jnp.float32) / modulus
    fixed_real = (far_real * ratio).astype(jnp.bfloat16)
    fixed_imag = (far_imag * ratio).astype(jnp.bfloat16)
    back_real, back_imag = left_apply(cos_table, -sin_table, fixed_real, fixed_imag)
    new_real, new_imag = right_apply(
        cos_table, -sin_table, back_real.astype(jnp.bfloat16), back_imag.astype(jnp.bfloat16)
    )
    slope_real = -absorb_col * wave_real - phase_col * wave_imag
    slope_imag = -absorb_col * wave_imag + phase_col * wave_real
    change_real = new_real - wave_real
    change_imag = new_imag - wave_imag
    weight_live = alive.astype(jnp.float32)[:, None, None]
    numerator = jnp.sum(slope_real * change_real + slope_imag * change_imag, axis=1) * weight_live
    weights = jnp.sum(slope_real * slope_real + slope_imag * slope_imag, axis=1) * weight_live
    return (numerator, weights)


def tile_max(value):
    count = lax.axis_size("tile")
    spread = jnp.broadcast_to(value, (count, 128))
    gathered = lax.all_to_all(spread, "tile", 0, 0, tiled=True)
    return jnp.max(gathered)


def move_rims(strips, offset):
    return passed_along(strips, "tile", offset)


def shards(thickness, illumination, absorb, phases, amplitudes, positions, batch_order, live_slots):
    tile_now = thickness[0]
    tile_height, tile_width = tile_now.shape
    window = illumination.shape[-1]
    slots = live_slots.shape[2]
    column = lax.axis_index("tile") % GRID_X
    keep_right = (column != GRID_X - 1).astype(jnp.float32)
    keep_left = (column != 0).astype(jnp.float32)
    cos_table, sin_table = tables(window)
    for batch_index in range(BATCHES):
        strip_right = move_rims(tile_now[None, :, :window], -1)[0] * keep_right
        widened = jnp.concatenate([tile_now, strip_right], 1)
        strip_below = move_rims(widened[None, :window, :], -GRID_X)[0]
        extended = jnp.concatenate([widened, strip_below], 0)
        chosen = batch_order[0, batch_index * slots : (batch_index + 1) * slots]
        places = positions[0][chosen]
        measured = amplitudes[0][chosen]
        alive = live_slots[0, batch_index]
        cells = jax.vmap(
            lambda place: lax.dynamic_slice(extended, (place[0], place[1]), (window, window))
        )(places)
        numer_win, weight_win = window_terms(
            cells, illumination, absorb, phases, measured, alive, cos_table, sin_table
        )
        numer_win, weight_win = lax.psum((numer_win, weight_win), "wave")

        def add_window(slot_index, totals):
            numer_map, weight_map = totals
            row_at = places[slot_index, 0]
            col_at = places[slot_index, 1]
            numer_map = lax.dynamic_update_slice(
                numer_map,
                lax.dynamic_slice(numer_map, (row_at, col_at), (window, window))
                + numer_win[slot_index],
                (row_at, col_at),
            )
            weight_map = lax.dynamic_update_slice(
                weight_map,
                lax.dynamic_slice(weight_map, (row_at, col_at), (window, window))
                + weight_win[slot_index],
                (row_at, col_at),
            )
            return (numer_map, weight_map)

        empty = jnp.zeros((tile_height + window, tile_width + window), jnp.float32)
        numer_map, weight_map = lax.fori_loop(0, slots, add_window, (empty, empty))
        stacked = jnp.stack([numer_map, weight_map])
        arrived_below = move_rims(stacked[:, tile_height:, :], GRID_X)
        folded = stacked[:, :tile_height, :].at[:, :window, :].add(arrived_below)
        arrived_side = move_rims(folded[:, :, tile_width:], 1) * keep_left
        maps = folded[:, :, :tile_width].at[:, :, :window].add(arrived_side)
        largest = tile_max(jnp.max(maps[1]))
        tile_now = tile_now + 0.5 * maps[0] / (0.75 * maps[1] + 0.25 * largest)
    return tile_now[None]


def solution(mesh):
    placed = (
        P("tile", None, None),
        P("wave", None, None, None),
        P("wave"),
        P("wave"),
        P("tile", None, "wave", None, None),
        P("tile", None, None),
        P("tile", None),
        P("tile", None, None),
    )
    return jax.shard_map(
        shards, mesh=mesh, in_specs=placed, out_specs=P("tile", None, None), check_vma=False
    )
```

```python
import math

import jax
import jax.numpy as jnp
from jax import lax
from jax.sharding import PartitionSpec as P

GRID_X = 8
BATCHES = 3


def tables(points):
    counter = jnp.arange(points, dtype=jnp.int32)
    angles = (
        2.0 * math.pi / points * (counter[:, None] * counter[None, :] % points).astype(jnp.float32)
    )
    factor = 1.0 / math.sqrt(points)
    return (
        (jnp.cos(angles) * factor).astype(jnp.bfloat16),
        (-jnp.sin(angles) * factor).astype(jnp.bfloat16),
    )


def left_apply(real_part, imag_part, left_real, left_imag):
    points = real_part.shape[0]
    stacked = jnp.concatenate([real_part, imag_part], 0)
    joined = jnp.concatenate([left_real, left_imag], -1)
    product = jnp.einsum("ij,...jk->...ik", stacked, joined, preferred_element_type=jnp.float32)
    return (
        product[..., :points, :points] - product[..., points:, points:],
        product[..., :points, points:] + product[..., points:, :points],
    )


def right_apply(real_part, imag_part, left_real, left_imag):
    points = real_part.shape[0]
    stacked = jnp.concatenate([real_part, imag_part], 1)
    joined = jnp.concatenate([left_real, left_imag], -2)
    product = jnp.einsum("...ij,jk->...ik", joined, stacked, preferred_element_type=jnp.float32)
    return (
        product[..., :points, :points] - product[..., points:, points:],
        product[..., :points, points:] + product[..., points:, :points],
    )


def window_terms(cells, illumination, absorb, phases, measured, alive, cos_table, sin_table):
    absorb_col = absorb[None, :, None, None]
    phase_col = phases[None, :, None, None]
    spread = cells[:, None, :, :]
    magnitude = jnp.exp(-absorb_col * spread)
    object_real = magnitude * jnp.cos(phase_col * spread)
    object_imag = magnitude * jnp.sin(phase_col * spread)
    probe_real = illumination[None, :, 0]
    probe_imag = illumination[None, :, 1]
    wave_real = probe_real * object_real - probe_imag * object_imag
    wave_imag = probe_real * object_imag + probe_imag * object_real
    half_real, half_imag = left_apply(
        cos_table, sin_table, wave_real.astype(jnp.bfloat16), wave_imag.astype(jnp.bfloat16)
    )
    far_real, far_imag = right_apply(
        cos_table, sin_table, half_real.astype(jnp.bfloat16), half_imag.astype(jnp.bfloat16)
    )
    modulus = jnp.sqrt(far_real * far_real + far_imag * far_imag + 0.25)
    ratio = measured.astype(jnp.float32) / modulus
    fixed_real = (far_real * ratio).astype(jnp.bfloat16)
    fixed_imag = (far_imag * ratio).astype(jnp.bfloat16)
    back_real, back_imag = left_apply(cos_table, -sin_table, fixed_real, fixed_imag)
    new_real, new_imag = right_apply(
        cos_table, -sin_table, back_real.astype(jnp.bfloat16), back_imag.astype(jnp.bfloat16)
    )
    slope_real = -absorb_col * wave_real - phase_col * wave_imag
    slope_imag = -absorb_col * wave_imag + phase_col * wave_real
    change_real = new_real - wave_real
    change_imag = new_imag - wave_imag
    weight_live = alive.astype(jnp.float32)[:, None, None]
    numerator = jnp.sum(slope_real * change_real + slope_imag * change_imag, axis=1) * weight_live
    weights = jnp.sum(slope_real * slope_real + slope_imag * slope_imag, axis=1) * weight_live
    return (numerator, weights)


def tile_max(value):
    count = lax.axis_size("tile")
    spread = jnp.broadcast_to(value, (count, 128))
    gathered = lax.all_to_all(spread, "tile", 0, 0, tiled=True)
    return jnp.max(gathered)


def from_offset(block, axis, distance):
    devices = range(lax.axis_size(axis))
    route = [(i + distance, i) for i in devices if i + distance in devices]
    return lax.ppermute(block, axis, route)


def partner(block, bit):
    return lax.ppermute(block, "wave", [(i, i ^ bit) for i in range(lax.axis_size("wave"))])


def wave_sum(maps):
    count = lax.axis_size("wave")
    rows = maps.shape[1] // 2
    odd = lax.axis_index("wave") % 2
    kept = lax.dynamic_slice_in_dim(maps, odd * rows, rows, axis=1)
    given = lax.dynamic_slice_in_dim(maps, (1 - odd) * rows, rows, axis=1)
    half = kept + partner(given, 1)
    bit = 2
    while bit < count:
        half = half + partner(half, bit)
        bit *= 2
    other = partner(half, 1)
    low = jnp.where(odd == 0, half, other)
    high = jnp.where(odd == 0, other, half)
    return jnp.concatenate([low, high], 1)


def picker(offsets, size, span):
    cells = lax.broadcasted_iota(jnp.int32, (offsets.shape[0], size, span), 1)
    spots = lax.broadcasted_iota(jnp.int32, (offsets.shape[0], size, span), 2)
    return (cells == spots + offsets[:, None, None]).astype(jnp.float32)


def shards(thickness, illumination, absorb, phases, amplitudes, positions, batch_order, live_slots):
    tile_now = thickness[0]
    tile_height, tile_width = tile_now.shape
    window = illumination.shape[-1]
    slots = live_slots.shape[2]
    column = lax.axis_index("tile") % GRID_X
    keep_right = (column != GRID_X - 1).astype(jnp.float32)
    keep_left = (column != 0).astype(jnp.float32)
    cos_table, sin_table = tables(window)
    exact = lax.Precision.HIGHEST
    for batch_index in range(BATCHES):
        right = from_offset(tile_now, "tile", 1) * keep_right
        below = from_offset(tile_now, "tile", GRID_X)
        corner = from_offset(tile_now, "tile", GRID_X + 1) * keep_right
        extended = jnp.concatenate(
            [jnp.concatenate([tile_now, right], 1), jnp.concatenate([below, corner], 1)], 0
        )
        chosen = batch_order[0, batch_index * slots : (batch_index + 1) * slots]
        places = positions[0][chosen]
        measured = amplitudes[0][chosen]
        alive = live_slots[0, batch_index]
        row_pick = picker(places[:, 0], tile_height + window, window)
        col_pick = picker(places[:, 1], tile_width + window, window)
        strips = jnp.einsum("sij,ik->sjk", row_pick, extended, precision=exact)
        cells = jnp.einsum("sjk,skl->sjl", strips, col_pick, precision=exact)
        numer_win, weight_win = window_terms(
            cells, illumination, absorb, phases, measured, alive, cos_table, sin_table
        )
        wins = jnp.stack([numer_win, weight_win], 1)
        placed_rows = jnp.einsum("sij,smjk->smik", row_pick, wins, precision=exact)
        spread = jnp.einsum("smik,slk->mil", placed_rows, col_pick, precision=exact)
        own = spread[:, :tile_height, :tile_width]
        from_left = from_offset(spread[:, :tile_height, tile_width:], "tile", -1) * keep_left
        from_above = from_offset(spread[:, tile_height:, :tile_width], "tile", -GRID_X)
        from_corner = (
            from_offset(spread[:, tile_height:, tile_width:], "tile", -GRID_X - 1) * keep_left
        )
        maps = wave_sum(own + from_left + from_above + from_corner)
        largest = tile_max(jnp.max(maps[1]))
        tile_now = tile_now + 0.5 * maps[0] / (0.75 * maps[1] + 0.25 * largest)
    return tile_now[None]


def solution(mesh):
    placed = (
        P("tile", None, None),
        P("wave", None, None, None),
        P("wave"),
        P("wave"),
        P("tile", None, "wave", None, None),
        P("tile", None, None),
        P("tile", None),
        P("tile", None, None),
    )
    return jax.shard_map(
        shards, mesh=mesh, in_specs=placed, out_specs=P("tile", None, None), check_vma=False
    )
```

```python
import math

import jax
import jax.numpy as jnp
from jax import lax
from jax.sharding import PartitionSpec as P

GRID_X = 8
BATCHES = 3


def tables(points):
    counter = jnp.arange(points, dtype=jnp.int32)
    angles = (
        2.0 * math.pi / points * (counter[:, None] * counter[None, :] % points).astype(jnp.float32)
    )
    factor = 1.0 / math.sqrt(points)
    return (
        (jnp.cos(angles) * factor).astype(jnp.bfloat16),
        (-jnp.sin(angles) * factor).astype(jnp.bfloat16),
    )


def left_apply(real_part, imag_part, left_real, left_imag):
    points = real_part.shape[0]
    stacked = jnp.concatenate([real_part, imag_part], 0)
    joined = jnp.concatenate([left_real, left_imag], -1)
    product = jnp.einsum("ij,...jk->...ik", stacked, joined, preferred_element_type=jnp.float32)
    return (
        product[..., :points, :points] - product[..., points:, points:],
        product[..., :points, points:] + product[..., points:, :points],
    )


def right_apply(real_part, imag_part, left_real, left_imag):
    points = real_part.shape[0]
    stacked = jnp.concatenate([real_part, imag_part], 1)
    joined = jnp.concatenate([left_real, left_imag], -2)
    product = jnp.einsum("...ij,jk->...ik", joined, stacked, preferred_element_type=jnp.float32)
    return (
        product[..., :points, :points] - product[..., points:, points:],
        product[..., :points, points:] + product[..., points:, :points],
    )


def window_terms(cells, illumination, absorb, phases, measured, alive, cos_table, sin_table):
    absorb_col = absorb[None, :, None, None]
    phase_col = phases[None, :, None, None]
    spread = cells[:, None, :, :]
    magnitude = jnp.exp(-absorb_col * spread)
    object_real = magnitude * jnp.cos(phase_col * spread)
    object_imag = magnitude * jnp.sin(phase_col * spread)
    probe_real = illumination[None, :, 0]
    probe_imag = illumination[None, :, 1]
    wave_real = probe_real * object_real - probe_imag * object_imag
    wave_imag = probe_real * object_imag + probe_imag * object_real
    half_real, half_imag = left_apply(
        cos_table, sin_table, wave_real.astype(jnp.bfloat16), wave_imag.astype(jnp.bfloat16)
    )
    far_real, far_imag = right_apply(
        cos_table, sin_table, half_real.astype(jnp.bfloat16), half_imag.astype(jnp.bfloat16)
    )
    modulus = jnp.sqrt(far_real * far_real + far_imag * far_imag + 0.25)
    ratio = measured.astype(jnp.float32) / modulus
    fixed_real = (far_real * ratio).astype(jnp.bfloat16)
    fixed_imag = (far_imag * ratio).astype(jnp.bfloat16)
    back_real, back_imag = left_apply(cos_table, -sin_table, fixed_real, fixed_imag)
    new_real, new_imag = right_apply(
        cos_table, -sin_table, back_real.astype(jnp.bfloat16), back_imag.astype(jnp.bfloat16)
    )
    slope_real = -absorb_col * wave_real - phase_col * wave_imag
    slope_imag = -absorb_col * wave_imag + phase_col * wave_real
    change_real = new_real - wave_real
    change_imag = new_imag - wave_imag
    weight_live = alive.astype(jnp.float32)[:, None, None]
    numerator = jnp.sum(slope_real * change_real + slope_imag * change_imag, axis=1) * weight_live
    weights = jnp.sum(slope_real * slope_real + slope_imag * slope_imag, axis=1) * weight_live
    return (numerator, weights)


def tile_max(value):
    count = lax.axis_size("tile")
    spread = jnp.broadcast_to(value, (count, 128))
    gathered = lax.all_to_all(spread, "tile", 0, 0, tiled=True)
    return jnp.max(gathered)


def from_offset(block, axis, distance):
    devices = range(lax.axis_size(axis))
    route = [(i + distance, i) for i in devices if i + distance in devices]
    return lax.ppermute(block, axis, route)


def partner(block, bit):
    return lax.ppermute(block, "wave", [(i, i ^ bit) for i in range(lax.axis_size("wave"))])


def wave_sum(maps):
    count = lax.axis_size("wave")
    rows = maps.shape[1] // 2
    odd = lax.axis_index("wave") % 2
    kept = lax.dynamic_slice_in_dim(maps, odd * rows, rows, axis=1)
    given = lax.dynamic_slice_in_dim(maps, (1 - odd) * rows, rows, axis=1)
    half = kept + partner(given, 1)
    bit = 2
    while bit < count:
        half = half + partner(half, bit)
        bit *= 2
    other = partner(half, 1)
    low = jnp.where(odd == 0, half, other)
    high = jnp.where(odd == 0, other, half)
    return jnp.concatenate([low, high], 1)


def picker(offsets, size, span):
    cells = lax.broadcasted_iota(jnp.int32, (offsets.shape[0], size, span), 1)
    spots = lax.broadcasted_iota(jnp.int32, (offsets.shape[0], size, span), 2)
    return (cells == spots + offsets[:, None, None]).astype(jnp.float32)


def shards(thickness, illumination, absorb, phases, amplitudes, positions, batch_order, live_slots):
    tile_now = thickness[0]
    tile_height, tile_width = tile_now.shape
    window = illumination.shape[-1]
    slots = live_slots.shape[2]
    column = lax.axis_index("tile") % GRID_X
    keep_right = (column != GRID_X - 1).astype(jnp.float32)
    keep_left = (column != 0).astype(jnp.float32)
    cos_table, sin_table = tables(window)
    exact = lax.Precision.HIGHEST
    right = from_offset(tile_now, "tile", 1) * keep_right
    below = from_offset(tile_now, "tile", GRID_X)
    corner = from_offset(tile_now, "tile", GRID_X + 1) * keep_right
    extended = jnp.concatenate(
        [jnp.concatenate([tile_now, right], 1), jnp.concatenate([below, corner], 1)], 0
    )
    for batch_index in range(BATCHES):
        chosen = batch_order[0, batch_index * slots : (batch_index + 1) * slots]
        places = positions[0][chosen]
        measured = amplitudes[0][chosen]
        alive = live_slots[0, batch_index]
        row_pick = picker(places[:, 0], tile_height + window, window)
        col_pick = picker(places[:, 1], tile_width + window, window)
        strips = jnp.einsum("sij,ik->sjk", row_pick, extended, precision=exact)
        cells = jnp.einsum("sjk,skl->sjl", strips, col_pick, precision=exact)
        numer_win, weight_win = window_terms(
            cells, illumination, absorb, phases, measured, alive, cos_table, sin_table
        )
        wins = jnp.stack([numer_win, weight_win], 1)
        placed_rows = jnp.einsum("sij,smjk->smik", row_pick, wins, precision=exact)
        spread = jnp.einsum("smik,slk->mil", placed_rows, col_pick, precision=exact)
        own = spread[:, :tile_height, :tile_width]
        from_left = from_offset(spread[:, :tile_height, tile_width:], "tile", -1) * keep_left
        from_above = from_offset(spread[:, tile_height:, :tile_width], "tile", -GRID_X)
        from_corner = (
            from_offset(spread[:, tile_height:, tile_width:], "tile", -GRID_X - 1) * keep_left
        )
        maps = wave_sum(own + from_left + from_above + from_corner)
        if batch_index + 1 < BATCHES:
            maps_right = from_offset(maps, "tile", 1) * keep_right
            maps_below = from_offset(maps, "tile", GRID_X)
            maps_corner = from_offset(maps, "tile", GRID_X + 1) * keep_right
            maps = jnp.concatenate(
                [
                    jnp.concatenate([maps, maps_right], 2),
                    jnp.concatenate([maps_below, maps_corner], 2),
                ],
                1,
            )
        largest = tile_max(jnp.max(maps[1, :tile_height, :tile_width]))
        if batch_index + 1 < BATCHES:
            extended = extended + 0.5 * maps[0] / (0.75 * maps[1] + 0.25 * largest)
            tile_now = extended[:tile_height, :tile_width]
        else:
            tile_now = tile_now + 0.5 * maps[0] / (0.75 * maps[1] + 0.25 * largest)
    return tile_now[None]


def solution(mesh):
    placed = (
        P("tile", None, None),
        P("wave", None, None, None),
        P("wave"),
        P("wave"),
        P("tile", None, "wave", None, None),
        P("tile", None, None),
        P("tile", None),
        P("tile", None, None),
    )
    return jax.shard_map(
        shards, mesh=mesh, in_specs=placed, out_specs=P("tile", None, None), check_vma=False
    )
```

```python
import math

import jax
import jax.numpy as jnp
from jax import lax
from jax.sharding import PartitionSpec as P

GRID_X = 8
BATCHES = 3


def tables(points):
    counter = jnp.arange(points, dtype=jnp.int32)
    angles = (
        2.0 * math.pi / points * (counter[:, None] * counter[None, :] % points).astype(jnp.float32)
    )
    factor = 1.0 / math.sqrt(points)
    return (
        (jnp.cos(angles) * factor).astype(jnp.bfloat16),
        (-jnp.sin(angles) * factor).astype(jnp.bfloat16),
    )


def left_apply(real_part, imag_part, left_real, left_imag):
    points = real_part.shape[0]
    stacked = jnp.concatenate([real_part, imag_part], 0)
    joined = jnp.concatenate([left_real, left_imag], -1)
    product = jnp.einsum("ij,...jk->...ik", stacked, joined, preferred_element_type=jnp.float32)
    return (
        product[..., :points, :points] - product[..., points:, points:],
        product[..., :points, points:] + product[..., points:, :points],
    )


def right_apply(real_part, imag_part, left_real, left_imag):
    points = real_part.shape[0]
    stacked = jnp.concatenate([real_part, imag_part], 1)
    joined = jnp.concatenate([left_real, left_imag], -2)
    product = jnp.einsum("...ij,jk->...ik", joined, stacked, preferred_element_type=jnp.float32)
    return (
        product[..., :points, :points] - product[..., points:, points:],
        product[..., :points, points:] + product[..., points:, :points],
    )


def window_terms(cells, illumination, absorb, phases, measured, alive, cos_table, sin_table):
    absorb_col = absorb[None, :, None, None]
    phase_col = phases[None, :, None, None]
    spread = cells[:, None, :, :]
    magnitude = jnp.exp(-absorb_col * spread)
    object_real = magnitude * jnp.cos(phase_col * spread)
    object_imag = magnitude * jnp.sin(phase_col * spread)
    probe_real = illumination[None, :, 0]
    probe_imag = illumination[None, :, 1]
    wave_real = probe_real * object_real - probe_imag * object_imag
    wave_imag = probe_real * object_imag + probe_imag * object_real
    half_real, half_imag = left_apply(
        cos_table, sin_table, wave_real.astype(jnp.bfloat16), wave_imag.astype(jnp.bfloat16)
    )
    far_real, far_imag = right_apply(
        cos_table, sin_table, half_real.astype(jnp.bfloat16), half_imag.astype(jnp.bfloat16)
    )
    modulus = jnp.sqrt(far_real * far_real + far_imag * far_imag + 0.25)
    ratio = measured.astype(jnp.float32) / modulus
    fixed_real = (far_real * ratio).astype(jnp.bfloat16)
    fixed_imag = (far_imag * ratio).astype(jnp.bfloat16)
    back_real, back_imag = left_apply(cos_table, -sin_table, fixed_real, fixed_imag)
    new_real, new_imag = right_apply(
        cos_table, -sin_table, back_real.astype(jnp.bfloat16), back_imag.astype(jnp.bfloat16)
    )
    slope_real = -absorb_col * wave_real - phase_col * wave_imag
    slope_imag = -absorb_col * wave_imag + phase_col * wave_real
    change_real = new_real - wave_real
    change_imag = new_imag - wave_imag
    weight_live = alive.astype(jnp.float32)[:, None, None]
    numerator = jnp.sum(slope_real * change_real + slope_imag * change_imag, axis=1) * weight_live
    weights = jnp.sum(slope_real * slope_real + slope_imag * slope_imag, axis=1) * weight_live
    return (numerator, weights)


def tile_max(value):
    count = lax.axis_size("tile")
    spread = jnp.broadcast_to(value, (count, 128))
    gathered = lax.all_to_all(spread, "tile", 0, 0, tiled=True)
    return jnp.max(gathered)


def from_tile(block, rows, columns):
    waves, tiles = lax.axis_size("wave"), lax.axis_size("tile")
    grid_rows = tiles // GRID_X
    half = GRID_X // 2
    pairs = []
    for target in range(tiles):
        row, col = target // GRID_X + rows, target % GRID_X + columns
        if not (0 <= row < grid_rows and 0 <= col < GRID_X):
            continue
        source = row * GRID_X + col
        crossing = (col // half) != ((target % GRID_X) // half)
        for wave in range(waves):
            giver = (waves // 2 - 1 - wave // 2) * 2 + wave % 2 if crossing else wave
            pairs.append((giver * tiles + source, wave * tiles + target))
    return lax.ppermute(block, ("wave", "tile"), pairs)


def partner(block, bit):
    return lax.ppermute(block, "wave", [(i, i ^ bit) for i in range(lax.axis_size("wave"))])


def wave_sum(maps):
    count = lax.axis_size("wave")
    rows = maps.shape[1] // 2
    odd = lax.axis_index("wave") % 2
    kept = lax.dynamic_slice_in_dim(maps, odd * rows, rows, axis=1)
    given = lax.dynamic_slice_in_dim(maps, (1 - odd) * rows, rows, axis=1)
    half = kept + partner(given, 1)
    bit = 2
    while bit < count:
        half = half + partner(half, bit)
        bit *= 2
    other = partner(half, 1)
    low = jnp.where(odd == 0, half, other)
    high = jnp.where(odd == 0, other, half)
    return jnp.concatenate([low, high], 1)


def picker(offsets, size, span):
    cells = lax.broadcasted_iota(jnp.int32, (offsets.shape[0], size, span), 1)
    spots = lax.broadcasted_iota(jnp.int32, (offsets.shape[0], size, span), 2)
    return (cells == spots + offsets[:, None, None]).astype(jnp.float32)


def shards(thickness, illumination, absorb, phases, amplitudes, positions, batch_order, live_slots):
    tile_now = thickness[0]
    tile_height, tile_width = tile_now.shape
    window = illumination.shape[-1]
    slots = live_slots.shape[2]
    cos_table, sin_table = tables(window)
    exact = lax.Precision.HIGHEST
    right = from_tile(tile_now, 0, 1)
    below = from_tile(tile_now, 1, 0)
    corner = from_tile(tile_now, 1, 1)
    extended = jnp.concatenate(
        [jnp.concatenate([tile_now, right], 1), jnp.concatenate([below, corner], 1)], 0
    )
    for batch_index in range(BATCHES):
        chosen = batch_order[0, batch_index * slots : (batch_index + 1) * slots]
        places = positions[0][chosen]
        measured = amplitudes[0][chosen]
        alive = live_slots[0, batch_index]
        row_pick = picker(places[:, 0], tile_height + window, window)
        col_pick = picker(places[:, 1], tile_width + window, window)
        strips = jnp.einsum("sij,ik->sjk", row_pick, extended, precision=exact)
        cells = jnp.einsum("sjk,skl->sjl", strips, col_pick, precision=exact)
        numer_win, weight_win = window_terms(
            cells, illumination, absorb, phases, measured, alive, cos_table, sin_table
        )
        wins = jnp.stack([numer_win, weight_win], 1)
        placed_rows = jnp.einsum("sij,smjk->smik", row_pick, wins, precision=exact)
        spread = jnp.einsum("smik,slk->mil", placed_rows, col_pick, precision=exact)
        own = spread[:, :tile_height, :tile_width]
        from_left = from_tile(spread[:, :tile_height, tile_width:], 0, -1)
        from_above = from_tile(spread[:, tile_height:, :tile_width], -1, 0)
        from_corner = (
            from_tile(spread[:, tile_height:, tile_width:], -1, -1)
        )
        maps = wave_sum(own + from_left + from_above + from_corner)
        if batch_index + 1 < BATCHES:
            maps_right = from_tile(maps, 0, 1)
            maps_below = from_tile(maps, 1, 0)
            maps_corner = from_tile(maps, 1, 1)
            maps = jnp.concatenate(
                [
                    jnp.concatenate([maps, maps_right], 2),
                    jnp.concatenate([maps_below, maps_corner], 2),
                ],
                1,
            )
        largest = tile_max(jnp.max(maps[1, :tile_height, :tile_width]))
        if batch_index + 1 < BATCHES:
            extended = extended + 0.5 * maps[0] / (0.75 * maps[1] + 0.25 * largest)
            tile_now = extended[:tile_height, :tile_width]
        else:
            tile_now = tile_now + 0.5 * maps[0] / (0.75 * maps[1] + 0.25 * largest)
    return tile_now[None]


def solution(mesh):
    placed = (
        P("tile", None, None),
        P("wave", None, None, None),
        P("wave"),
        P("wave"),
        P("tile", None, "wave", None, None),
        P("tile", None, None),
        P("tile", None),
        P("tile", None, None),
    )
    return jax.shard_map(
        shards, mesh=mesh, in_specs=placed, out_specs=P("tile", None, None), check_vma=False
    )
```

```python
import math

import jax
import jax.numpy as jnp
from jax import lax
from jax.sharding import PartitionSpec as P

GRID_X = 8
BATCHES = 3


def tables(points):
    counter = jnp.arange(points, dtype=jnp.int32)
    angles = (
        2.0 * math.pi / points * (counter[:, None] * counter[None, :] % points).astype(jnp.float32)
    )
    factor = 1.0 / math.sqrt(points)
    return (
        (jnp.cos(angles) * factor).astype(jnp.bfloat16),
        (-jnp.sin(angles) * factor).astype(jnp.bfloat16),
    )


def left_apply(real_part, imag_part, left_real, left_imag):
    points = real_part.shape[0]
    stacked = jnp.concatenate([real_part, imag_part], 0)
    joined = jnp.concatenate([left_real, left_imag], -1)
    product = jnp.einsum("ij,...jk->...ik", stacked, joined, preferred_element_type=jnp.float32)
    return (
        product[..., :points, :points] - product[..., points:, points:],
        product[..., :points, points:] + product[..., points:, :points],
    )


def right_apply(real_part, imag_part, left_real, left_imag):
    points = real_part.shape[0]
    stacked = jnp.concatenate([real_part, imag_part], 1)
    joined = jnp.concatenate([left_real, left_imag], -2)
    product = jnp.einsum("...ij,jk->...ik", joined, stacked, preferred_element_type=jnp.float32)
    return (
        product[..., :points, :points] - product[..., points:, points:],
        product[..., :points, points:] + product[..., points:, :points],
    )


def window_terms(cells, illumination, absorb, phases, measured, alive, cos_table, sin_table):
    absorb_col = absorb[None, :, None, None]
    phase_col = phases[None, :, None, None]
    spread = cells[:, None, :, :]
    magnitude = jnp.exp(-absorb_col * spread)
    object_real = magnitude * jnp.cos(phase_col * spread)
    object_imag = magnitude * jnp.sin(phase_col * spread)
    probe_real = illumination[None, :, 0]
    probe_imag = illumination[None, :, 1]
    wave_real = probe_real * object_real - probe_imag * object_imag
    wave_imag = probe_real * object_imag + probe_imag * object_real
    half_real, half_imag = left_apply(
        cos_table, sin_table, wave_real.astype(jnp.bfloat16), wave_imag.astype(jnp.bfloat16)
    )
    far_real, far_imag = right_apply(
        cos_table, sin_table, half_real.astype(jnp.bfloat16), half_imag.astype(jnp.bfloat16)
    )
    modulus = jnp.sqrt(far_real * far_real + far_imag * far_imag + 0.25)
    ratio = measured.astype(jnp.float32) / modulus
    fixed_real = (far_real * ratio).astype(jnp.bfloat16)
    fixed_imag = (far_imag * ratio).astype(jnp.bfloat16)
    back_real, back_imag = left_apply(cos_table, -sin_table, fixed_real, fixed_imag)
    new_real, new_imag = right_apply(
        cos_table, -sin_table, back_real.astype(jnp.bfloat16), back_imag.astype(jnp.bfloat16)
    )
    slope_real = -absorb_col * wave_real - phase_col * wave_imag
    slope_imag = -absorb_col * wave_imag + phase_col * wave_real
    change_real = new_real - wave_real
    change_imag = new_imag - wave_imag
    weight_live = alive.astype(jnp.float32)[:, None, None]
    numerator = jnp.sum(slope_real * change_real + slope_imag * change_imag, axis=1) * weight_live
    weights = jnp.sum(slope_real * slope_real + slope_imag * slope_imag, axis=1) * weight_live
    return (numerator, weights)


def tile_max(value):
    count = lax.axis_size("tile")
    spread = jnp.broadcast_to(value, (count, 128))
    gathered = lax.all_to_all(spread, "tile", 0, 0, tiled=True)
    return jnp.max(gathered)


def from_tile(block, rows, columns):
    waves, tiles = lax.axis_size("wave"), lax.axis_size("tile")
    grid_rows = tiles // GRID_X
    half = GRID_X // 2
    pairs = []
    for target in range(tiles):
        row, col = target // GRID_X + rows, target % GRID_X + columns
        if not (0 <= row < grid_rows and 0 <= col < GRID_X):
            continue
        source = row * GRID_X + col
        crossing = (col // half) != ((target % GRID_X) // half)
        for wave in range(waves):
            giver = (waves // 2 - 1 - wave // 2) * 2 + wave % 2 if crossing else wave
            pairs.append((giver * tiles + source, wave * tiles + target))
    return lax.ppermute(block, ("wave", "tile"), pairs)


def partner(block, bit):
    return lax.ppermute(block, "wave", [(i, i ^ bit) for i in range(lax.axis_size("wave"))])


def wave_sum(maps):
    count = lax.axis_size("wave")
    rows = maps.shape[1] // 2
    odd = lax.axis_index("wave") % 2
    kept = lax.dynamic_slice_in_dim(maps, odd * rows, rows, axis=1)
    given = lax.dynamic_slice_in_dim(maps, (1 - odd) * rows, rows, axis=1)
    half = kept + partner(given, 1)
    bit = 2
    while bit < count:
        half = half + partner(half, bit)
        bit *= 2
    other = partner(half, 1)
    low = jnp.where(odd == 0, half, other)
    high = jnp.where(odd == 0, other, half)
    return jnp.concatenate([low, high], 1)


def picker(offsets, size, span):
    cells = lax.broadcasted_iota(jnp.int32, (offsets.shape[0], size, span), 1)
    spots = lax.broadcasted_iota(jnp.int32, (offsets.shape[0], size, span), 2)
    return (cells == spots + offsets[:, None, None]).astype(jnp.float32)


def shards(thickness, illumination, absorb, phases, amplitudes, positions, batch_order, live_slots):
    tile_now = thickness[0]
    tile_height, tile_width = tile_now.shape
    window = illumination.shape[-1]
    slots = live_slots.shape[2]
    cos_table, sin_table = tables(window)
    exact = lax.Precision.HIGHEST
    for batch_index in range(BATCHES):
        right = from_tile(tile_now, 0, 1)
        below = from_tile(tile_now, 1, 0)
        corner = from_tile(tile_now, 1, 1)
        extended = jnp.concatenate(
            [jnp.concatenate([tile_now, right], 1), jnp.concatenate([below, corner], 1)], 0
        )
        chosen = batch_order[0, batch_index * slots : (batch_index + 1) * slots]
        places = positions[0][chosen]
        measured = amplitudes[0][chosen]
        alive = live_slots[0, batch_index]
        row_pick = picker(places[:, 0], tile_height + window, window)
        col_pick = picker(places[:, 1], tile_width + window, window)
        strips = jnp.einsum("sij,ik->sjk", row_pick, extended, precision=exact)
        cells = jnp.einsum("sjk,skl->sjl", strips, col_pick, precision=exact)
        numer_win, weight_win = window_terms(
            cells, illumination, absorb, phases, measured, alive, cos_table, sin_table
        )
        wins = jnp.stack([numer_win, weight_win], 1)
        placed_rows = jnp.einsum("sij,smjk->smik", row_pick, wins, precision=exact)
        spread = jnp.einsum("smik,slk->mil", placed_rows, col_pick, precision=exact)
        own = spread[:, :tile_height, :tile_width]
        from_left = from_tile(spread[:, :tile_height, tile_width:], 0, -1)
        from_above = from_tile(spread[:, tile_height:, :tile_width], -1, 0)
        from_corner = (
            from_tile(spread[:, tile_height:, tile_width:], -1, -1)
        )
        maps = wave_sum(own + from_left + from_above + from_corner)
        largest = tile_max(jnp.max(maps[1]))
        tile_now = tile_now + 0.5 * maps[0] / (0.75 * maps[1] + 0.25 * largest)
    return tile_now[None]


def solution(mesh):
    placed = (
        P("tile", None, None),
        P("wave", None, None, None),
        P("wave"),
        P("wave"),
        P("tile", None, "wave", None, None),
        P("tile", None, None),
        P("tile", None),
        P("tile", None, None),
    )
    return jax.shard_map(
        shards, mesh=mesh, in_specs=placed, out_specs=P("tile", None, None), check_vma=False
    )
```

```python
import math

import jax
import jax.numpy as jnp
from jax import lax
from jax.sharding import PartitionSpec as P

GRID_X = 8
BATCHES = 3


def tables(points):
    counter = jnp.arange(points, dtype=jnp.int32)
    angles = (
        2.0 * math.pi / points * (counter[:, None] * counter[None, :] % points).astype(jnp.float32)
    )
    factor = 1.0 / math.sqrt(points)
    return (
        (jnp.cos(angles) * factor).astype(jnp.bfloat16),
        (-jnp.sin(angles) * factor).astype(jnp.bfloat16),
    )


def left_apply(real_part, imag_part, left_real, left_imag):
    points = real_part.shape[0]
    stacked = jnp.concatenate([real_part, imag_part], 0)
    joined = jnp.concatenate([left_real, left_imag], -1)
    product = jnp.einsum("ij,...jk->...ik", stacked, joined, preferred_element_type=jnp.float32)
    return (
        product[..., :points, :points] - product[..., points:, points:],
        product[..., :points, points:] + product[..., points:, :points],
    )


def right_apply(real_part, imag_part, left_real, left_imag):
    points = real_part.shape[0]
    stacked = jnp.concatenate([real_part, imag_part], 1)
    joined = jnp.concatenate([left_real, left_imag], -2)
    product = jnp.einsum("...ij,jk->...ik", joined, stacked, preferred_element_type=jnp.float32)
    return (
        product[..., :points, :points] - product[..., points:, points:],
        product[..., :points, points:] + product[..., points:, :points],
    )


def over_waves(terms):
    total = terms[:, 0]
    for wave in range(1, terms.shape[1]):
        total = total + terms[:, wave]
    return total


def split_exact(values):
    high = values.astype(jnp.bfloat16)
    rest = values - high.astype(jnp.float32)
    middle = rest.astype(jnp.bfloat16)
    low = (rest - middle.astype(jnp.float32)).astype(jnp.bfloat16)
    return jnp.stack([high, middle, low])


def pick(spec, picker_matrix, values, picker_first):
    parts = split_exact(values)
    ones = picker_matrix.astype(jnp.bfloat16)
    if picker_first:
        moved = jnp.einsum(spec, ones, parts, preferred_element_type=jnp.float32)
    else:
        moved = jnp.einsum(spec, parts, ones, preferred_element_type=jnp.float32)
    return (moved[0] + moved[1]) + moved[2]


def window_terms(cells, illumination, absorb, phases, measured, alive, cos_table, sin_table):
    absorb_col = absorb[None, :, None, None]
    phase_col = phases[None, :, None, None]
    spread = cells[:, None, :, :]
    magnitude = jnp.exp(-absorb_col * spread)
    object_real = magnitude * jnp.cos(phase_col * spread)
    object_imag = magnitude * jnp.sin(phase_col * spread)
    probe_real = illumination[None, :, 0]
    probe_imag = illumination[None, :, 1]
    wave_real = probe_real * object_real - probe_imag * object_imag
    wave_imag = probe_real * object_imag + probe_imag * object_real
    half_real, half_imag = left_apply(
        cos_table, sin_table, wave_real.astype(jnp.bfloat16), wave_imag.astype(jnp.bfloat16)
    )
    far_real, far_imag = right_apply(
        cos_table, sin_table, half_real.astype(jnp.bfloat16), half_imag.astype(jnp.bfloat16)
    )
    modulus = jnp.sqrt(far_real * far_real + far_imag * far_imag + 0.25)
    ratio = measured.astype(jnp.float32) / modulus
    fixed_real = (far_real * ratio).astype(jnp.bfloat16)
    fixed_imag = (far_imag * ratio).astype(jnp.bfloat16)
    back_real, back_imag = left_apply(cos_table, -sin_table, fixed_real, fixed_imag)
    new_real, new_imag = right_apply(
        cos_table, -sin_table, back_real.astype(jnp.bfloat16), back_imag.astype(jnp.bfloat16)
    )
    wave_real, wave_imag = lax.optimization_barrier((wave_real, wave_imag))
    slope_real = -absorb_col * wave_real - phase_col * wave_imag
    slope_imag = -absorb_col * wave_imag + phase_col * wave_real
    change_real = new_real - wave_real
    change_imag = new_imag - wave_imag
    weight_live = alive.astype(jnp.float32)[:, None, None]
    numerator = over_waves(slope_real * change_real + slope_imag * change_imag) * weight_live
    weights = over_waves(slope_real * slope_real + slope_imag * slope_imag) * weight_live
    return (numerator, weights)


def tile_max(value):
    count = lax.axis_size("tile")
    spread = jnp.broadcast_to(value, (count, 128))
    gathered = lax.all_to_all(spread, "tile", 0, 0, tiled=True)
    return jnp.max(gathered)


def from_tile(block, rows, columns):
    waves, tiles = lax.axis_size("wave"), lax.axis_size("tile")
    grid_rows = tiles // GRID_X
    half = GRID_X // 2
    pairs = []
    for target in range(tiles):
        row, col = target // GRID_X + rows, target % GRID_X + columns
        if not (0 <= row < grid_rows and 0 <= col < GRID_X):
            continue
        source = row * GRID_X + col
        crossing = (col // half) != ((target % GRID_X) // half)
        for wave in range(waves):
            giver = (waves // 2 - 1 - wave // 2) * 2 + wave % 2 if crossing else wave
            pairs.append((giver * tiles + source, wave * tiles + target))
    return lax.ppermute(block, ("wave", "tile"), pairs)


def partner(block, bit):
    return lax.ppermute(block, "wave", [(i, i ^ bit) for i in range(lax.axis_size("wave"))])


def wave_sum(maps):
    count = lax.axis_size("wave")
    rows = maps.shape[1] // 2
    odd = lax.axis_index("wave") % 2
    kept = lax.dynamic_slice_in_dim(maps, odd * rows, rows, axis=1)
    given = lax.dynamic_slice_in_dim(maps, (1 - odd) * rows, rows, axis=1)
    half = kept + partner(given, 1)
    bit = 2
    while bit < count:
        half = half + partner(half, bit)
        bit *= 2
    other = partner(half, 1)
    low = jnp.where(odd == 0, half, other)
    high = jnp.where(odd == 0, other, half)
    return jnp.concatenate([low, high], 1)


def picker(offsets, size, span):
    cells = lax.broadcasted_iota(jnp.int32, (offsets.shape[0], size, span), 1)
    spots = lax.broadcasted_iota(jnp.int32, (offsets.shape[0], size, span), 2)
    return (cells == spots + offsets[:, None, None]).astype(jnp.float32)


def shards(thickness, illumination, absorb, phases, amplitudes, positions, batch_order, live_slots):
    tile_now = thickness[0]
    tile_height, tile_width = tile_now.shape
    window = illumination.shape[-1]
    slots = live_slots.shape[2]
    cos_table, sin_table = tables(window)
    right = from_tile(tile_now, 0, 1)
    below = from_tile(tile_now, 1, 0)
    corner = from_tile(tile_now, 1, 1)
    extended = jnp.concatenate(
        [jnp.concatenate([tile_now, right], 1), jnp.concatenate([below, corner], 1)], 0
    )
    for batch_index in range(BATCHES):
        chosen = batch_order[0, batch_index * slots : (batch_index + 1) * slots]
        places = positions[0][chosen]
        measured = amplitudes[0][chosen]
        alive = live_slots[0, batch_index]
        row_pick = picker(places[:, 0], tile_height + window, window)
        col_pick = picker(places[:, 1], tile_width + window, window)
        strips = pick("sij,pik->psjk", row_pick, extended, True)
        cells = pick("psjk,skl->psjl", col_pick, strips, False)
        numer_win, weight_win = window_terms(
            cells, illumination, absorb, phases, measured, alive, cos_table, sin_table
        )
        wins = jnp.stack([numer_win, weight_win], 1)
        placed_rows = pick("sij,psmjk->psmik", row_pick, wins, True)
        spread = pick("psmik,slk->pmil", col_pick, placed_rows, False)
        own = spread[:, :tile_height, :tile_width]
        from_left = from_tile(spread[:, :tile_height, tile_width:], 0, -1)
        from_above = from_tile(spread[:, tile_height:, :tile_width], -1, 0)
        from_corner = (
            from_tile(spread[:, tile_height:, tile_width:], -1, -1)
        )
        maps = wave_sum(own + from_left + from_above + from_corner)
        if batch_index + 1 < BATCHES:
            maps_right = from_tile(maps, 0, 1)
            maps_below = from_tile(maps, 1, 0)
            maps_corner = from_tile(maps, 1, 1)
            maps = jnp.concatenate(
                [
                    jnp.concatenate([maps, maps_right], 2),
                    jnp.concatenate([maps_below, maps_corner], 2),
                ],
                1,
            )
        largest = tile_max(jnp.max(maps[1, :tile_height, :tile_width]))
        if batch_index + 1 < BATCHES:
            extended = extended + 0.5 * maps[0] / (0.75 * maps[1] + 0.25 * largest)
            tile_now = extended[:tile_height, :tile_width]
        else:
            tile_now = tile_now + 0.5 * maps[0] / (0.75 * maps[1] + 0.25 * largest)
    return tile_now[None]


def solution(mesh):
    placed = (
        P("tile", None, None),
        P("wave", None, None, None),
        P("wave"),
        P("wave"),
        P("tile", None, "wave", None, None),
        P("tile", None, None),
        P("tile", None),
        P("tile", None, None),
    )
    return jax.shard_map(
        shards, mesh=mesh, in_specs=placed, out_specs=P("tile", None, None), check_vma=False
    )
```

```python
import math

import jax
import jax.numpy as jnp
from jax import lax
from jax.sharding import PartitionSpec as P

GRID_X = 8
BATCHES = 3


def tables(points):
    counter = jnp.arange(points, dtype=jnp.int32)
    angles = (
        2.0 * math.pi / points * (counter[:, None] * counter[None, :] % points).astype(jnp.float32)
    )
    factor = 1.0 / math.sqrt(points)
    return (
        (jnp.cos(angles) * factor).astype(jnp.bfloat16),
        (-jnp.sin(angles) * factor).astype(jnp.bfloat16),
    )


def left_apply(real_part, imag_part, left_real, left_imag):
    points = real_part.shape[0]
    stacked = jnp.concatenate([real_part, imag_part], 0)
    joined = jnp.concatenate([left_real, left_imag], -1)
    product = jnp.einsum("ij,...jk->...ik", stacked, joined, preferred_element_type=jnp.float32)
    return (
        product[..., :points, :points] - product[..., points:, points:],
        product[..., :points, points:] + product[..., points:, :points],
    )


def right_apply(real_part, imag_part, left_real, left_imag):
    points = real_part.shape[0]
    stacked = jnp.concatenate([real_part, imag_part], 1)
    joined = jnp.concatenate([left_real, left_imag], -2)
    product = jnp.einsum("...ij,jk->...ik", joined, stacked, preferred_element_type=jnp.float32)
    return (
        product[..., :points, :points] - product[..., points:, points:],
        product[..., :points, points:] + product[..., points:, :points],
    )


def over_waves(terms):
    total = terms[:, 0]
    for wave in range(1, terms.shape[1]):
        total = total + terms[:, wave]
    return total


def split_exact(values):
    high = lax.reduce_precision(values, exponent_bits=8, mantissa_bits=7)
    rest = values - high
    middle = lax.reduce_precision(rest, exponent_bits=8, mantissa_bits=7)
    low = rest - middle
    return jnp.stack([high, middle, low]).astype(jnp.bfloat16)


def pick(spec, picker_matrix, values, picker_first):
    parts = split_exact(values)
    ones = picker_matrix.astype(jnp.bfloat16)
    if picker_first:
        moved = jnp.einsum(spec, ones, parts, preferred_element_type=jnp.float32)
    else:
        moved = jnp.einsum(spec, parts, ones, preferred_element_type=jnp.float32)
    return (moved[0] + moved[1]) + moved[2]


def window_terms(cells, illumination, absorb, phases, measured, alive, cos_table, sin_table):
    absorb_col = absorb[None, :, None, None]
    phase_col = phases[None, :, None, None]
    spread = cells[:, None, :, :]
    magnitude = jnp.exp(-absorb_col * spread)
    object_real = magnitude * jnp.cos(phase_col * spread)
    object_imag = magnitude * jnp.sin(phase_col * spread)
    probe_real = illumination[None, :, 0]
    probe_imag = illumination[None, :, 1]
    wave_real = probe_real * object_real - probe_imag * object_imag
    wave_imag = probe_real * object_imag + probe_imag * object_real
    half_real, half_imag = left_apply(
        cos_table, sin_table, wave_real.astype(jnp.bfloat16), wave_imag.astype(jnp.bfloat16)
    )
    far_real, far_imag = right_apply(
        cos_table, sin_table, half_real.astype(jnp.bfloat16), half_imag.astype(jnp.bfloat16)
    )
    modulus = jnp.sqrt(far_real * far_real + far_imag * far_imag + 0.25)
    ratio = measured.astype(jnp.float32) / modulus
    fixed_real = (far_real * ratio).astype(jnp.bfloat16)
    fixed_imag = (far_imag * ratio).astype(jnp.bfloat16)
    back_real, back_imag = left_apply(cos_table, -sin_table, fixed_real, fixed_imag)
    new_real, new_imag = right_apply(
        cos_table, -sin_table, back_real.astype(jnp.bfloat16), back_imag.astype(jnp.bfloat16)
    )
    wave_real, wave_imag = lax.optimization_barrier((wave_real, wave_imag))
    slope_real = -absorb_col * wave_real - phase_col * wave_imag
    slope_imag = -absorb_col * wave_imag + phase_col * wave_real
    change_real = new_real - wave_real
    change_imag = new_imag - wave_imag
    weight_live = alive.astype(jnp.float32)[:, None, None]
    numerator = over_waves(slope_real * change_real + slope_imag * change_imag) * weight_live
    weights = over_waves(slope_real * slope_real + slope_imag * slope_imag) * weight_live
    return (numerator, weights)


def tile_max(value):
    count = lax.axis_size("tile")
    spread = jnp.broadcast_to(value, (count, 128))
    gathered = lax.all_to_all(spread, "tile", 0, 0, tiled=True)
    return jnp.max(gathered)


def from_tile(block, rows, columns):
    waves, tiles = lax.axis_size("wave"), lax.axis_size("tile")
    grid_rows = tiles // GRID_X
    half = GRID_X // 2
    pairs = []
    for target in range(tiles):
        row, col = target // GRID_X + rows, target % GRID_X + columns
        if not (0 <= row < grid_rows and 0 <= col < GRID_X):
            continue
        source = row * GRID_X + col
        crossing = (col // half) != ((target % GRID_X) // half)
        for wave in range(waves):
            giver = (waves // 2 - 1 - wave // 2) * 2 + wave % 2 if crossing else wave
            pairs.append((giver * tiles + source, wave * tiles + target))
    return lax.ppermute(block, ("wave", "tile"), pairs)


def partner(block, bit):
    return lax.ppermute(block, "wave", [(i, i ^ bit) for i in range(lax.axis_size("wave"))])


def z_sum(block):
    bit = 2
    while bit < lax.axis_size("wave"):
        block = block + partner(block, bit)
        bit *= 2
    return block


def join_halves(block, core):
    other = partner(block, 1)
    low = jnp.where(core == 0, block, other)
    high = jnp.where(core == 0, other, block)
    return jnp.concatenate([low, high], -2)


def picker(offsets, size, span):
    cells = lax.broadcasted_iota(jnp.int32, (offsets.shape[0], size, span), 1)
    spots = lax.broadcasted_iota(jnp.int32, (offsets.shape[0], size, span), 2)
    return (cells == spots + offsets[:, None, None]).astype(jnp.float32)


def shards(thickness, illumination, absorb, phases, amplitudes, positions, batch_order, live_slots):
    tile_now = thickness[0]
    tile_height, tile_width = tile_now.shape
    window = illumination.shape[-1]
    slots = live_slots.shape[2]
    cos_table, sin_table = tables(window)
    right = from_tile(tile_now, 0, 1)
    below = from_tile(tile_now, 1, 0)
    corner = from_tile(tile_now, 1, 1)
    extended = jnp.concatenate(
        [jnp.concatenate([tile_now, right], 1), jnp.concatenate([below, corner], 1)], 0
    )
    for batch_index in range(BATCHES):
        chosen = batch_order[0, batch_index * slots : (batch_index + 1) * slots]
        places = positions[0][chosen]
        measured = amplitudes[0][chosen]
        alive = live_slots[0, batch_index]
        row_pick = picker(places[:, 0], tile_height + window, window)
        col_pick = picker(places[:, 1], tile_width + window, window)
        strips = pick("sij,pik->psjk", row_pick, extended, True)
        cells = pick("psjk,skl->psjl", col_pick, strips, False)
        numer_win, weight_win = window_terms(
            cells, illumination, absorb, phases, measured, alive, cos_table, sin_table
        )
        wins = jnp.stack([numer_win, weight_win], 1)
        placed_rows = pick("sij,psmjk->psmik", row_pick, wins, True)
        spread = pick("psmik,slk->pmil", col_pick, placed_rows, False)
        half = tile_height // 2
        core = lax.axis_index("wave") % 2
        quadrants = jnp.stack(
            [
                spread[:, :tile_height, :tile_width],
                spread[:, :tile_height, tile_width:],
                spread[:, tile_height:, :tile_width],
                spread[:, tile_height:, tile_width:],
            ]
        )
        kept = lax.dynamic_slice_in_dim(quadrants, core * half, half, axis=2)
        given = lax.dynamic_slice_in_dim(quadrants, (1 - core) * half, half, axis=2)
        quadrants = kept + partner(given, 1)
        own = quadrants[0]
        from_left = from_tile(quadrants[1], 0, -1)
        from_above = from_tile(quadrants[2], -1, 0)
        from_corner = from_tile(quadrants[3], -1, -1)
        halves = z_sum(own + from_left + from_above + from_corner)
        maps = join_halves(halves, core)
        largest = tile_max(jnp.max(maps[1]))
        if batch_index + 1 < BATCHES:
            around = jnp.stack(
                [from_tile(halves, 0, 1), from_tile(halves, 1, 0), from_tile(halves, 1, 1)]
            )
            around = join_halves(around, core)
            maps = jnp.concatenate(
                [
                    jnp.concatenate([maps, around[0]], 2),
                    jnp.concatenate([around[1], around[2]], 2),
                ],
                1,
            )
            extended = extended + 0.5 * maps[0] / (0.75 * maps[1] + 0.25 * largest)
            tile_now = extended[:tile_height, :tile_width]
        else:
            tile_now = tile_now + 0.5 * maps[0] / (0.75 * maps[1] + 0.25 * largest)
    return tile_now[None]


def solution(mesh):
    placed = (
        P("tile", None, None),
        P("wave", None, None, None),
        P("wave"),
        P("wave"),
        P("tile", None, "wave", None, None),
        P("tile", None, None),
        P("tile", None),
        P("tile", None, None),
    )
    return jax.shard_map(
        shards, mesh=mesh, in_specs=placed, out_specs=P("tile", None, None), check_vma=False
    )
```

```python
import math

import jax
import jax.numpy as jnp
from jax import lax
from jax.sharding import PartitionSpec as P

GRID_X = 8
BATCHES = 3


def tables(points):
    counter = jnp.arange(points, dtype=jnp.int32)
    angles = (
        2.0 * math.pi / points * (counter[:, None] * counter[None, :] % points).astype(jnp.float32)
    )
    factor = 1.0 / math.sqrt(points)
    return (
        (jnp.cos(angles) * factor).astype(jnp.bfloat16),
        (-jnp.sin(angles) * factor).astype(jnp.bfloat16),
    )


def left_apply(real_part, imag_part, left_real, left_imag):
    points = real_part.shape[0]
    stacked = jnp.concatenate([real_part, imag_part], 0)
    joined = jnp.concatenate([left_real, left_imag], -1)
    product = jnp.einsum("ij,...jk->...ik", stacked, joined, preferred_element_type=jnp.float32)
    return (
        product[..., :points, :points] - product[..., points:, points:],
        product[..., :points, points:] + product[..., points:, :points],
    )


def right_apply(real_part, imag_part, left_real, left_imag):
    points = real_part.shape[0]
    stacked = jnp.concatenate([real_part, imag_part], 1)
    joined = jnp.concatenate([left_real, left_imag], -2)
    product = jnp.einsum("...ij,jk->...ik", joined, stacked, preferred_element_type=jnp.float32)
    return (
        product[..., :points, :points] - product[..., points:, points:],
        product[..., :points, points:] + product[..., points:, :points],
    )


def over_waves(terms):
    total = terms[:, 0]
    for wave in range(1, terms.shape[1]):
        total = total + terms[:, wave]
    return total


def split_exact(values):
    high = lax.reduce_precision(values, exponent_bits=8, mantissa_bits=7)
    rest = values - high
    middle = lax.reduce_precision(rest, exponent_bits=8, mantissa_bits=7)
    low = rest - middle
    return jnp.stack([high, middle, low]).astype(jnp.bfloat16)


def pick(spec, picker_matrix, values, picker_first):
    parts = split_exact(values)
    ones = picker_matrix.astype(jnp.bfloat16)
    if picker_first:
        moved = jnp.einsum(spec, ones, parts, preferred_element_type=jnp.float32)
    else:
        moved = jnp.einsum(spec, parts, ones, preferred_element_type=jnp.float32)
    return (moved[0] + moved[1]) + moved[2]


def window_terms(cells, illumination, absorb, phases, measured, alive, cos_table, sin_table):
    absorb_col = absorb[None, :, None, None]
    phase_col = phases[None, :, None, None]
    spread = cells[:, None, :, :]
    magnitude = jnp.exp(-absorb_col * spread)
    object_real = magnitude * jnp.cos(phase_col * spread)
    object_imag = magnitude * jnp.sin(phase_col * spread)
    probe_real = illumination[None, :, 0]
    probe_imag = illumination[None, :, 1]
    wave_real = probe_real * object_real - probe_imag * object_imag
    wave_imag = probe_real * object_imag + probe_imag * object_real
    half_real, half_imag = left_apply(
        cos_table, sin_table, wave_real.astype(jnp.bfloat16), wave_imag.astype(jnp.bfloat16)
    )
    far_real, far_imag = right_apply(
        cos_table, sin_table, half_real.astype(jnp.bfloat16), half_imag.astype(jnp.bfloat16)
    )
    modulus = jnp.sqrt(far_real * far_real + far_imag * far_imag + 0.25)
    ratio = measured.astype(jnp.float32) / modulus
    fixed_real = (far_real * ratio).astype(jnp.bfloat16)
    fixed_imag = (far_imag * ratio).astype(jnp.bfloat16)
    back_real, back_imag = left_apply(cos_table, -sin_table, fixed_real, fixed_imag)
    new_real, new_imag = right_apply(
        cos_table, -sin_table, back_real.astype(jnp.bfloat16), back_imag.astype(jnp.bfloat16)
    )
    wave_real, wave_imag = lax.optimization_barrier((wave_real, wave_imag))
    slope_real = -absorb_col * wave_real - phase_col * wave_imag
    slope_imag = -absorb_col * wave_imag + phase_col * wave_real
    change_real = new_real - wave_real
    change_imag = new_imag - wave_imag
    weight_live = alive.astype(jnp.float32)[:, None, None]
    numerator = over_waves(slope_real * change_real + slope_imag * change_imag) * weight_live
    weights = over_waves(slope_real * slope_real + slope_imag * slope_imag) * weight_live
    return (numerator, weights)


def tile_max(value):
    count = lax.axis_size("tile")
    spread = jnp.broadcast_to(value, (count, 128))
    gathered = lax.all_to_all(spread, "tile", 0, 0, tiled=True)
    return jnp.max(gathered)


def from_tile(block, rows, columns):
    waves, tiles = lax.axis_size("wave"), lax.axis_size("tile")
    grid_rows = tiles // GRID_X
    half = GRID_X // 2
    pairs = []
    for target in range(tiles):
        row, col = target // GRID_X + rows, target % GRID_X + columns
        if not (0 <= row < grid_rows and 0 <= col < GRID_X):
            continue
        source = row * GRID_X + col
        crossing = (col // half) != ((target % GRID_X) // half)
        for wave in range(waves):
            giver = (waves // 2 - 1 - wave // 2) * 2 + wave % 2 if crossing else wave
            pairs.append((giver * tiles + source, wave * tiles + target))
    return lax.ppermute(block, ("wave", "tile"), pairs)


def partner(block, bit):
    return lax.ppermute(block, "wave", [(i, i ^ bit) for i in range(lax.axis_size("wave"))])


def z_sum(block):
    bit = 2
    while bit < lax.axis_size("wave"):
        block = block + partner(block, bit)
        bit *= 2
    return block


def join_halves(block, core):
    other = partner(block, 1)
    low = jnp.where(core == 0, block, other)
    high = jnp.where(core == 0, other, block)
    return jnp.concatenate([low, high], -2)


def picker(offsets, size, span):
    cells = lax.broadcasted_iota(jnp.int32, (offsets.shape[0], size, span), 1)
    spots = lax.broadcasted_iota(jnp.int32, (offsets.shape[0], size, span), 2)
    return (cells == spots + offsets[:, None, None]).astype(jnp.float32)


def shards(thickness, illumination, absorb, phases, amplitudes, positions, batch_order, live_slots):
    tile_now = thickness[0]
    tile_height, tile_width = tile_now.shape
    window = illumination.shape[-1]
    slots = live_slots.shape[2]
    cos_table, sin_table = tables(window)
    core = lax.axis_index("wave") % 2
    half = tile_height // 2
    rows = lax.dynamic_slice_in_dim(tile_now, core * half, half, axis=0)
    halo = jnp.stack([from_tile(rows, 0, 1), from_tile(rows, 1, 0), from_tile(rows, 1, 1)])
    right, below, corner = join_halves(halo, core)
    extended = jnp.concatenate(
        [jnp.concatenate([tile_now, right], 1), jnp.concatenate([below, corner], 1)], 0
    )
    for batch_index in range(BATCHES):
        chosen = batch_order[0, batch_index * slots : (batch_index + 1) * slots]
        places = positions[0][chosen]
        measured = amplitudes[0][chosen]
        alive = live_slots[0, batch_index]
        row_pick = picker(places[:, 0], tile_height + window, window)
        col_pick = picker(places[:, 1], tile_width + window, window)
        strips = pick("sij,pik->psjk", row_pick, extended, True)
        cells = pick("psjk,skl->psjl", col_pick, strips, False)
        numer_win, weight_win = window_terms(
            cells, illumination, absorb, phases, measured, alive, cos_table, sin_table
        )
        wins = jnp.stack([numer_win, weight_win], 1)
        placed_rows = pick("sij,psmjk->psmik", row_pick, wins, True)
        spread = pick("psmik,slk->pmil", col_pick, placed_rows, False)
        quadrants = jnp.stack(
            [
                spread[:, :tile_height, :tile_width],
                spread[:, :tile_height, tile_width:],
                spread[:, tile_height:, :tile_width],
                spread[:, tile_height:, tile_width:],
            ]
        )
        kept = lax.dynamic_slice_in_dim(quadrants, core * half, half, axis=2)
        given = lax.dynamic_slice_in_dim(quadrants, (1 - core) * half, half, axis=2)
        quadrants = kept + partner(given, 1)
        own = quadrants[0]
        from_left = from_tile(quadrants[1], 0, -1)
        from_above = from_tile(quadrants[2], -1, 0)
        from_corner = from_tile(quadrants[3], -1, -1)
        halves = z_sum(own + from_left + from_above + from_corner)
        maps = join_halves(halves, core)
        largest = tile_max(jnp.max(maps[1]))
        if batch_index + 1 < BATCHES:
            around = jnp.stack(
                [from_tile(halves, 0, 1), from_tile(halves, 1, 0), from_tile(halves, 1, 1)]
            )
            around = join_halves(around + 0.0 * largest, core)
            maps = jnp.concatenate(
                [
                    jnp.concatenate([maps, around[0]], 2),
                    jnp.concatenate([around[1], around[2]], 2),
                ],
                1,
            )
            extended = extended + 0.5 * maps[0] / (0.75 * maps[1] + 0.25 * largest)
            tile_now = extended[:tile_height, :tile_width]
        else:
            tile_now = tile_now + 0.5 * maps[0] / (0.75 * maps[1] + 0.25 * largest)
    return tile_now[None]


def solution(mesh):
    placed = (
        P("tile", None, None),
        P("wave", None, None, None),
        P("wave"),
        P("wave"),
        P("tile", None, "wave", None, None),
        P("tile", None, None),
        P("tile", None),
        P("tile", None, None),
    )
    return jax.shard_map(
        shards, mesh=mesh, in_specs=placed, out_specs=P("tile", None, None), check_vma=False
    )
```

```python
import math

import jax
import jax.numpy as jnp
from jax import lax
from jax.sharding import PartitionSpec as P

GRID_X = 8
BATCHES = 3


def tables(points):
    counter = jnp.arange(points, dtype=jnp.int32)
    angles = (
        2.0 * math.pi / points * (counter[:, None] * counter[None, :] % points).astype(jnp.float32)
    )
    factor = 1.0 / math.sqrt(points)
    return (
        (jnp.cos(angles) * factor).astype(jnp.bfloat16),
        (-jnp.sin(angles) * factor).astype(jnp.bfloat16),
    )


def left_apply(real_part, imag_part, left_real, left_imag):
    points = real_part.shape[0]
    stacked = jnp.concatenate([real_part, imag_part], 0)
    joined = jnp.concatenate([left_real, left_imag], -1)
    product = jnp.einsum("ij,...jk->...ik", stacked, joined, preferred_element_type=jnp.float32)
    return (
        product[..., :points, :points] - product[..., points:, points:],
        product[..., :points, points:] + product[..., points:, :points],
    )


def right_apply(real_part, imag_part, left_real, left_imag):
    points = real_part.shape[0]
    stacked = jnp.concatenate([real_part, imag_part], 1)
    joined = jnp.concatenate([left_real, left_imag], -2)
    product = jnp.einsum("...ij,jk->...ik", joined, stacked, preferred_element_type=jnp.float32)
    return (
        product[..., :points, :points] - product[..., points:, points:],
        product[..., :points, points:] + product[..., points:, :points],
    )


def over_waves(terms):
    total = terms[:, 0]
    for wave in range(1, terms.shape[1]):
        total = total + terms[:, wave]
    return total


def split_exact(values):
    high = lax.reduce_precision(values, exponent_bits=8, mantissa_bits=7)
    rest = values - high
    middle = lax.reduce_precision(rest, exponent_bits=8, mantissa_bits=7)
    low = rest - middle
    return jnp.stack([high, middle, low]).astype(jnp.bfloat16)


def pick(spec, picker_matrix, values, picker_first):
    parts = split_exact(values)
    ones = picker_matrix.astype(jnp.bfloat16)
    if picker_first:
        moved = jnp.einsum(spec, ones, parts, preferred_element_type=jnp.float32)
    else:
        moved = jnp.einsum(spec, parts, ones, preferred_element_type=jnp.float32)
    return (moved[0] + moved[1]) + moved[2]


def window_terms(cells, illumination, absorb, phases, measured, alive, cos_table, sin_table):
    absorb_col = absorb[None, :, None, None]
    phase_col = phases[None, :, None, None]
    spread = cells[:, None, :, :]
    magnitude = jnp.exp(-absorb_col * spread)
    object_real = magnitude * jnp.cos(phase_col * spread)
    object_imag = magnitude * jnp.sin(phase_col * spread)
    probe_real = illumination[None, :, 0]
    probe_imag = illumination[None, :, 1]
    wave_real = probe_real * object_real - probe_imag * object_imag
    wave_imag = probe_real * object_imag + probe_imag * object_real
    half_real, half_imag = left_apply(
        cos_table, sin_table, wave_real.astype(jnp.bfloat16), wave_imag.astype(jnp.bfloat16)
    )
    far_real, far_imag = right_apply(
        cos_table, sin_table, half_real.astype(jnp.bfloat16), half_imag.astype(jnp.bfloat16)
    )
    modulus = jnp.sqrt(far_real * far_real + far_imag * far_imag + 0.25)
    ratio = measured.astype(jnp.float32) / modulus
    fixed_real = (far_real * ratio).astype(jnp.bfloat16)
    fixed_imag = (far_imag * ratio).astype(jnp.bfloat16)
    back_real, back_imag = left_apply(cos_table, -sin_table, fixed_real, fixed_imag)
    new_real, new_imag = right_apply(
        cos_table, -sin_table, back_real.astype(jnp.bfloat16), back_imag.astype(jnp.bfloat16)
    )
    wave_real, wave_imag = lax.optimization_barrier((wave_real, wave_imag))
    slope_real = -absorb_col * wave_real - phase_col * wave_imag
    slope_imag = -absorb_col * wave_imag + phase_col * wave_real
    change_real = new_real - wave_real
    change_imag = new_imag - wave_imag
    weight_live = alive.astype(jnp.float32)[:, None, None]
    numerator = over_waves(slope_real * change_real + slope_imag * change_imag) * weight_live
    weights = over_waves(slope_real * slope_real + slope_imag * slope_imag) * weight_live
    return (numerator, weights)


def tile_max(value):
    count = lax.axis_size("tile")
    spread = jnp.broadcast_to(value, (count, 128))
    gathered = lax.all_to_all(spread, "tile", 0, 0, tiled=True)
    return jnp.max(gathered)


def from_tile(block, rows, columns):
    waves, tiles = lax.axis_size("wave"), lax.axis_size("tile")
    grid_rows = tiles // GRID_X
    half = GRID_X // 2
    pairs = []
    for target in range(tiles):
        row, col = target // GRID_X + rows, target % GRID_X + columns
        if not (0 <= row < grid_rows and 0 <= col < GRID_X):
            continue
        source = row * GRID_X + col
        crossing = (col // half) != ((target % GRID_X) // half)
        for wave in range(waves):
            giver = (waves // 2 - 1 - wave // 2) * 2 + wave % 2 if crossing else wave
            pairs.append((giver * tiles + source, wave * tiles + target))
    return lax.ppermute(block, ("wave", "tile"), pairs)


def partner(block, bit):
    return lax.ppermute(block, "wave", [(i, i ^ bit) for i in range(lax.axis_size("wave"))])


def z_sum(block):
    bit = 2
    while bit < lax.axis_size("wave"):
        block = block + partner(block, bit)
        bit *= 2
    return block


def join_halves(block, core):
    other = partner(block, 1)
    low = jnp.where(core == 0, block, other)
    high = jnp.where(core == 0, other, block)
    return jnp.concatenate([low, high], -2)


def picker(offsets, size, span):
    cells = lax.broadcasted_iota(jnp.int32, (offsets.shape[0], size, span), 1)
    spots = lax.broadcasted_iota(jnp.int32, (offsets.shape[0], size, span), 2)
    return (cells == spots + offsets[:, None, None]).astype(jnp.float32)


def shards(thickness, illumination, absorb, phases, amplitudes, positions, batch_order, live_slots):
    tile_now = thickness[0]
    tile_height, tile_width = tile_now.shape
    window = illumination.shape[-1]
    slots = live_slots.shape[2]
    cos_table, sin_table = tables(window)
    core = lax.axis_index("wave") % 2
    half = tile_height // 2
    rows = lax.dynamic_slice_in_dim(tile_now, core * half, half, axis=0)
    halo = jnp.stack([from_tile(rows, 0, 1), from_tile(rows, 1, 0), from_tile(rows, 1, 1)])
    right, below, corner = join_halves(halo, core)
    extended = jnp.concatenate(
        [jnp.concatenate([tile_now, right], 1), jnp.concatenate([below, corner], 1)], 0
    )
    for batch_index in range(BATCHES):
        chosen = batch_order[0, batch_index * slots : (batch_index + 1) * slots]
        places = positions[0][chosen]
        measured = amplitudes[0][chosen]
        alive = live_slots[0, batch_index]
        row_pick = picker(places[:, 0], tile_height + window, window)
        col_pick = picker(places[:, 1], tile_width + window, window)
        strips = pick("sij,pik->psjk", row_pick, extended, True)
        cells = pick("psjk,skl->psjl", col_pick, strips, False)
        numer_win, weight_win = window_terms(
            cells, illumination, absorb, phases, measured, alive, cos_table, sin_table
        )
        wins = jnp.stack([numer_win, weight_win], 1)
        placed_rows = pick("sij,psmjk->psmik", row_pick, wins, True)
        spread = pick("psmik,slk->pmil", col_pick, placed_rows, False)
        quadrants = jnp.stack(
            [
                spread[:, :tile_height, :tile_width],
                spread[:, :tile_height, tile_width:],
                spread[:, tile_height:, :tile_width],
                spread[:, tile_height:, tile_width:],
            ]
        )
        kept = lax.dynamic_slice_in_dim(quadrants, core * half, half, axis=2)
        given = lax.dynamic_slice_in_dim(quadrants, (1 - core) * half, half, axis=2)
        quadrants = kept + partner(given, 1)
        own = quadrants[0]
        from_left = from_tile(quadrants[1], 0, -1)
        from_above = from_tile(quadrants[2], -1, 0)
        from_corner = from_tile(quadrants[3], -1, -1)
        halves = z_sum(own + from_left + from_above + from_corner)
        maps = join_halves(halves, core)
        largest = tile_max(jnp.max(maps[1]))
        if batch_index + 1 < BATCHES:
            around = jnp.stack([from_tile(halves, 0, 1), from_tile(halves, 1, 0)])
            around = join_halves(around + 0.0 * largest, core)
            maps = jnp.concatenate([jnp.stack([maps, around[0]]), around[1][None]])
            near = jnp.stack([tile_now, extended[:tile_height, tile_width:], extended[tile_height:, :tile_width]])
            near = near + 0.5 * maps[:, 0] / (0.75 * maps[:, 1] + 0.25 * largest)
            tile_now = near[0]
            rows = lax.dynamic_slice_in_dim(tile_now, core * half, half, axis=0)
            corner = join_halves(from_tile(rows, 1, 1), core)
            extended = jnp.concatenate(
                [jnp.concatenate([near[0], near[1]], 1), jnp.concatenate([near[2], corner], 1)], 0
            )
        else:
            tile_now = tile_now + 0.5 * maps[0] / (0.75 * maps[1] + 0.25 * largest)
    return tile_now[None]


def solution(mesh):
    placed = (
        P("tile", None, None),
        P("wave", None, None, None),
        P("wave"),
        P("wave"),
        P("tile", None, "wave", None, None),
        P("tile", None, None),
        P("tile", None),
        P("tile", None, None),
    )
    return jax.shard_map(
        shards, mesh=mesh, in_specs=placed, out_specs=P("tile", None, None), check_vma=False
    )
```

```python
import math

import jax
import jax.numpy as jnp
from jax import lax
from jax.sharding import PartitionSpec as P

GRID_X = 8
BATCHES = 3


def tables(points):
    counter = jnp.arange(points, dtype=jnp.int32)
    angles = (
        2.0 * math.pi / points * (counter[:, None] * counter[None, :] % points).astype(jnp.float32)
    )
    factor = 1.0 / math.sqrt(points)
    return (
        (jnp.cos(angles) * factor).astype(jnp.bfloat16),
        (-jnp.sin(angles) * factor).astype(jnp.bfloat16),
    )


def left_apply(real_part, imag_part, left_real, left_imag):
    points = real_part.shape[0]
    stacked = jnp.concatenate([real_part, imag_part], 0)
    joined = jnp.concatenate([left_real, left_imag], -1)
    product = jnp.einsum("ij,...jk->...ik", stacked, joined, preferred_element_type=jnp.float32)
    return (
        product[..., :points, :points] - product[..., points:, points:],
        product[..., :points, points:] + product[..., points:, :points],
    )


def right_apply(real_part, imag_part, left_real, left_imag):
    points = real_part.shape[0]
    stacked = jnp.concatenate([real_part, imag_part], 1)
    joined = jnp.concatenate([left_real, left_imag], -2)
    product = jnp.einsum("...ij,jk->...ik", joined, stacked, preferred_element_type=jnp.float32)
    return (
        product[..., :points, :points] - product[..., points:, points:],
        product[..., :points, points:] + product[..., points:, :points],
    )


def over_waves(terms):
    total = terms[:, 0]
    for wave in range(1, terms.shape[1]):
        total = total + terms[:, wave]
    return total


def split_exact(values):
    high = lax.reduce_precision(values, exponent_bits=8, mantissa_bits=7)
    rest = values - high
    middle = lax.reduce_precision(rest, exponent_bits=8, mantissa_bits=7)
    low = rest - middle
    return jnp.stack([high, middle, low]).astype(jnp.bfloat16)


def pick(spec, picker_matrix, values, picker_first):
    parts = split_exact(values)
    ones = picker_matrix.astype(jnp.bfloat16)
    if picker_first:
        moved = jnp.einsum(spec, ones, parts, preferred_element_type=jnp.float32)
    else:
        moved = jnp.einsum(spec, parts, ones, preferred_element_type=jnp.float32)
    return (moved[0] + moved[1]) + moved[2]


def window_terms(cells, illumination, absorb, phases, measured, alive, cos_table, sin_table):
    absorb_col = absorb[None, :, None, None]
    phase_col = phases[None, :, None, None]
    spread = cells[:, None, :, :]
    magnitude = jnp.exp(-absorb_col * spread)
    object_real = magnitude * jnp.cos(phase_col * spread)
    object_imag = magnitude * jnp.sin(phase_col * spread)
    probe_real = illumination[None, :, 0]
    probe_imag = illumination[None, :, 1]
    wave_real = probe_real * object_real - probe_imag * object_imag
    wave_imag = probe_real * object_imag + probe_imag * object_real
    half_real, half_imag = left_apply(
        cos_table, sin_table, wave_real.astype(jnp.bfloat16), wave_imag.astype(jnp.bfloat16)
    )
    far_real, far_imag = right_apply(
        cos_table, sin_table, half_real.astype(jnp.bfloat16), half_imag.astype(jnp.bfloat16)
    )
    modulus = jnp.sqrt(far_real * far_real + far_imag * far_imag + 0.25)
    ratio = measured.astype(jnp.float32) / modulus
    fixed_real = (far_real * ratio).astype(jnp.bfloat16)
    fixed_imag = (far_imag * ratio).astype(jnp.bfloat16)
    back_real, back_imag = left_apply(cos_table, -sin_table, fixed_real, fixed_imag)
    new_real, new_imag = right_apply(
        cos_table, -sin_table, back_real.astype(jnp.bfloat16), back_imag.astype(jnp.bfloat16)
    )
    wave_real, wave_imag = lax.optimization_barrier((wave_real, wave_imag))
    slope_real = -absorb_col * wave_real - phase_col * wave_imag
    slope_imag = -absorb_col * wave_imag + phase_col * wave_real
    change_real = new_real - wave_real
    change_imag = new_imag - wave_imag
    weight_live = alive.astype(jnp.float32)[:, None, None]
    numerator = over_waves(slope_real * change_real + slope_imag * change_imag) * weight_live
    weights = over_waves(slope_real * slope_real + slope_imag * slope_imag) * weight_live
    return (numerator, weights)


def tile_max(value):
    count = lax.axis_size("tile")
    spread = jnp.broadcast_to(value, (count, 128))
    gathered = lax.all_to_all(spread, "tile", 0, 0, tiled=True)
    return jnp.max(gathered)


def from_tile(block, rows, columns):
    waves, tiles = lax.axis_size("wave"), lax.axis_size("tile")
    grid_rows = tiles // GRID_X
    half = GRID_X // 2
    pairs = []
    for target in range(tiles):
        row, col = target // GRID_X + rows, target % GRID_X + columns
        if not (0 <= row < grid_rows and 0 <= col < GRID_X):
            continue
        source = row * GRID_X + col
        crossing = (col // half) != ((target % GRID_X) // half)
        for wave in range(waves):
            giver = (waves // 2 - 1 - wave // 2) * 2 + wave % 2 if crossing else wave
            pairs.append((giver * tiles + source, wave * tiles + target))
    return lax.ppermute(block, ("wave", "tile"), pairs)


def partner(block, bit):
    return lax.ppermute(block, "wave", [(i, i ^ bit) for i in range(lax.axis_size("wave"))])


def z_sum(block):
    bit = 2
    while bit < lax.axis_size("wave"):
        block = block + partner(block, bit)
        bit *= 2
    return block


def fold_sum(quadrants):
    own = quadrants[0]
    from_left = from_tile(quadrants[1], 0, -1)
    from_above = from_tile(quadrants[2], -1, 0)
    from_corner = from_tile(quadrants[3], -1, -1)
    return z_sum(own + from_left + from_above + from_corner)


def join_halves(block, core):
    other = partner(block, 1)
    low = jnp.where(core == 0, block, other)
    high = jnp.where(core == 0, other, block)
    return jnp.concatenate([low, high], -2)


def picker(offsets, size, span):
    cells = lax.broadcasted_iota(jnp.int32, (offsets.shape[0], size, span), 1)
    spots = lax.broadcasted_iota(jnp.int32, (offsets.shape[0], size, span), 2)
    return (cells == spots + offsets[:, None, None]).astype(jnp.float32)


def shards(thickness, illumination, absorb, phases, amplitudes, positions, batch_order, live_slots):
    tile_now = thickness[0]
    tile_height, tile_width = tile_now.shape
    window = illumination.shape[-1]
    slots = live_slots.shape[2]
    cos_table, sin_table = tables(window)
    core = lax.axis_index("wave") % 2
    half = tile_height // 2
    rows = lax.dynamic_slice_in_dim(tile_now, core * half, half, axis=0)
    halo = jnp.stack([from_tile(rows, 0, 1), from_tile(rows, 1, 0), from_tile(rows, 1, 1)])
    right, below, corner = join_halves(halo, core)
    extended = jnp.concatenate(
        [jnp.concatenate([tile_now, right], 1), jnp.concatenate([below, corner], 1)], 0
    )
    for batch_index in range(BATCHES):
        chosen = batch_order[0, batch_index * slots : (batch_index + 1) * slots]
        places = positions[0][chosen]
        measured = amplitudes[0][chosen]
        alive = live_slots[0, batch_index]
        row_pick = picker(places[:, 0], tile_height + window, window)
        col_pick = picker(places[:, 1], tile_width + window, window)
        strips = pick("sij,pik->psjk", row_pick, extended, True)
        cells = pick("psjk,skl->psjl", col_pick, strips, False)
        numer_win, weight_win = window_terms(
            cells, illumination, absorb, phases, measured, alive, cos_table, sin_table
        )
        wins = jnp.stack([numer_win, weight_win], 1)
        placed_rows = pick("sij,psmjk->psmik", row_pick, wins, True)
        spread = pick("psmik,slk->pmil", col_pick, placed_rows, False)
        quadrants = jnp.stack(
            [
                spread[:, :tile_height, :tile_width],
                spread[:, :tile_height, tile_width:],
                spread[:, tile_height:, :tile_width],
                spread[:, tile_height:, tile_width:],
            ]
        )
        kept = lax.dynamic_slice_in_dim(quadrants, core * half, half, axis=2)
        given = lax.dynamic_slice_in_dim(quadrants, (1 - core) * half, half, axis=2)
        quadrants = kept + partner(given, 1)
        weight_half = fold_sum(quadrants[:, 1])
        weight = join_halves(weight_half, core)
        largest = tile_max(jnp.max(weight))
        numer_half = fold_sum(quadrants[:, 0])
        halves = jnp.stack([numer_half, weight_half])
        maps = jnp.stack([join_halves(numer_half, core), weight])
        if batch_index + 1 < BATCHES:
            around = jnp.stack(
                [from_tile(halves, 0, 1), from_tile(halves, 1, 0), from_tile(halves, 1, 1)]
            )
            around = join_halves(around + 0.0 * largest, core)
            maps = jnp.concatenate(
                [
                    jnp.concatenate([maps, around[0]], 2),
                    jnp.concatenate([around[1], around[2]], 2),
                ],
                1,
            )
            extended = extended + 0.5 * maps[0] / (0.75 * maps[1] + 0.25 * largest)
            tile_now = extended[:tile_height, :tile_width]
        else:
            tile_now = tile_now + 0.5 * maps[0] / (0.75 * maps[1] + 0.25 * largest)
    return tile_now[None]


def solution(mesh):
    placed = (
        P("tile", None, None),
        P("wave", None, None, None),
        P("wave"),
        P("wave"),
        P("tile", None, "wave", None, None),
        P("tile", None, None),
        P("tile", None),
        P("tile", None, None),
    )
    return jax.shard_map(
        shards, mesh=mesh, in_specs=placed, out_specs=P("tile", None, None), check_vma=False
    )
```

```python
import math

import jax
import jax.numpy as jnp
from jax import lax
from jax.sharding import PartitionSpec as P

GRID_X = 8
BATCHES = 3


def tables(points):
    counter = jnp.arange(points, dtype=jnp.int32)
    angles = (
        2.0 * math.pi / points * (counter[:, None] * counter[None, :] % points).astype(jnp.float32)
    )
    factor = 1.0 / math.sqrt(points)
    return (
        (jnp.cos(angles) * factor).astype(jnp.bfloat16),
        (-jnp.sin(angles) * factor).astype(jnp.bfloat16),
    )


def left_apply(real_part, imag_part, left_real, left_imag):
    points = real_part.shape[0]
    stacked = jnp.concatenate([real_part, imag_part], 0)
    joined = jnp.concatenate([left_real, left_imag], -1)
    product = jnp.einsum("ij,...jk->...ik", stacked, joined, preferred_element_type=jnp.float32)
    return (
        product[..., :points, :points] - product[..., points:, points:],
        product[..., :points, points:] + product[..., points:, :points],
    )


def right_apply(real_part, imag_part, left_real, left_imag):
    points = real_part.shape[0]
    stacked = jnp.concatenate([real_part, imag_part], 1)
    joined = jnp.concatenate([left_real, left_imag], -2)
    product = jnp.einsum("...ij,jk->...ik", joined, stacked, preferred_element_type=jnp.float32)
    return (
        product[..., :points, :points] - product[..., points:, points:],
        product[..., :points, points:] + product[..., points:, :points],
    )


def over_waves(terms):
    total = terms[:, 0]
    for wave in range(1, terms.shape[1]):
        total = total + terms[:, wave]
    return total


def split_exact(values):
    high = lax.reduce_precision(values, exponent_bits=8, mantissa_bits=7)
    rest = values - high
    middle = lax.reduce_precision(rest, exponent_bits=8, mantissa_bits=7)
    low = rest - middle
    return jnp.stack([high, middle, low]).astype(jnp.bfloat16)


def pick(spec, picker_matrix, values, picker_first):
    parts = split_exact(values)
    ones = picker_matrix.astype(jnp.bfloat16)
    if picker_first:
        moved = jnp.einsum(spec, ones, parts, preferred_element_type=jnp.float32)
    else:
        moved = jnp.einsum(spec, parts, ones, preferred_element_type=jnp.float32)
    return (moved[0] + moved[1]) + moved[2]


def window_terms(cells, illumination, absorb, phases, measured, alive, cos_table, sin_table):
    absorb_col = absorb[None, :, None, None]
    phase_col = phases[None, :, None, None]
    spread = cells[:, None, :, :]
    magnitude = jnp.exp(-absorb_col * spread)
    object_real = magnitude * jnp.cos(phase_col * spread)
    object_imag = magnitude * jnp.sin(phase_col * spread)
    probe_real = illumination[None, :, 0]
    probe_imag = illumination[None, :, 1]
    wave_real = probe_real * object_real - probe_imag * object_imag
    wave_imag = probe_real * object_imag + probe_imag * object_real
    half_real, half_imag = left_apply(
        cos_table, sin_table, wave_real.astype(jnp.bfloat16), wave_imag.astype(jnp.bfloat16)
    )
    far_real, far_imag = right_apply(
        cos_table, sin_table, half_real.astype(jnp.bfloat16), half_imag.astype(jnp.bfloat16)
    )
    modulus = jnp.sqrt(far_real * far_real + far_imag * far_imag + 0.25)
    ratio = measured.astype(jnp.float32) / modulus
    fixed_real = (far_real * ratio).astype(jnp.bfloat16)
    fixed_imag = (far_imag * ratio).astype(jnp.bfloat16)
    back_real, back_imag = left_apply(cos_table, -sin_table, fixed_real, fixed_imag)
    new_real, new_imag = right_apply(
        cos_table, -sin_table, back_real.astype(jnp.bfloat16), back_imag.astype(jnp.bfloat16)
    )
    wave_real, wave_imag = lax.optimization_barrier((wave_real, wave_imag))
    slope_real = -absorb_col * wave_real - phase_col * wave_imag
    slope_imag = -absorb_col * wave_imag + phase_col * wave_real
    change_real = new_real - wave_real
    change_imag = new_imag - wave_imag
    weight_live = alive.astype(jnp.float32)[:, None, None]
    numerator = over_waves(slope_real * change_real + slope_imag * change_imag) * weight_live
    weights = over_waves(slope_real * slope_real + slope_imag * slope_imag) * weight_live
    return (numerator, weights)


def tile_max(value):
    count = lax.axis_size("tile")
    spread = jnp.broadcast_to(value, (count, 128))
    gathered = lax.all_to_all(spread, "tile", 0, 0, tiled=True)
    return jnp.max(gathered)


def from_tile(block, rows, columns):
    waves, tiles = lax.axis_size("wave"), lax.axis_size("tile")
    grid_rows = tiles // GRID_X
    half = GRID_X // 2
    pairs = []
    for target in range(tiles):
        row, col = target // GRID_X + rows, target % GRID_X + columns
        if not (0 <= row < grid_rows and 0 <= col < GRID_X):
            continue
        source = row * GRID_X + col
        crossing = (col // half) != ((target % GRID_X) // half)
        for wave in range(waves):
            giver = ((wave // 2 + 2) % (waves // 2)) * 2 + wave % 2 if crossing else wave
            pairs.append((giver * tiles + source, wave * tiles + target))
    return lax.ppermute(block, ("wave", "tile"), pairs)


def partner(block, bit):
    return lax.ppermute(block, "wave", [(i, i ^ bit) for i in range(lax.axis_size("wave"))])


def z_sum(block):
    bit = 2
    while bit < lax.axis_size("wave"):
        block = block + partner(block, bit)
        bit *= 2
    return block


def join_halves(block, core):
    other = partner(block, 1)
    low = jnp.where(core == 0, block, other)
    high = jnp.where(core == 0, other, block)
    return jnp.concatenate([low, high], -2)


def picker(offsets, size, span):
    cells = lax.broadcasted_iota(jnp.int32, (offsets.shape[0], size, span), 1)
    spots = lax.broadcasted_iota(jnp.int32, (offsets.shape[0], size, span), 2)
    return (cells == spots + offsets[:, None, None]).astype(jnp.float32)


def shards(thickness, illumination, absorb, phases, amplitudes, positions, batch_order, live_slots):
    tile_now = thickness[0]
    tile_height, tile_width = tile_now.shape
    window = illumination.shape[-1]
    slots = live_slots.shape[2]
    cos_table, sin_table = tables(window)
    core = lax.axis_index("wave") % 2
    half = tile_height // 2
    rows = lax.dynamic_slice_in_dim(tile_now, core * half, half, axis=0)
    halo = jnp.stack([from_tile(rows, 0, 1), from_tile(rows, 1, 0), from_tile(rows, 1, 1)])
    right, below, corner = join_halves(halo, core)
    extended = jnp.concatenate(
        [jnp.concatenate([tile_now, right], 1), jnp.concatenate([below, corner], 1)], 0
    )
    for batch_index in range(BATCHES):
        chosen = batch_order[0, batch_index * slots : (batch_index + 1) * slots]
        places = positions[0][chosen]
        measured = amplitudes[0][chosen]
        alive = live_slots[0, batch_index]
        row_pick = picker(places[:, 0], tile_height + window, window)
        col_pick = picker(places[:, 1], tile_width + window, window)
        strips = pick("sij,pik->psjk", row_pick, extended, True)
        cells = pick("psjk,skl->psjl", col_pick, strips, False)
        numer_win, weight_win = window_terms(
            cells, illumination, absorb, phases, measured, alive, cos_table, sin_table
        )
        wins = jnp.stack([numer_win, weight_win], 1)
        placed_rows = pick("sij,psmjk->psmik", row_pick, wins, True)
        spread = pick("psmik,slk->pmil", col_pick, placed_rows, False)
        quadrants = jnp.stack(
            [
                spread[:, :tile_height, :tile_width],
                spread[:, :tile_height, tile_width:],
                spread[:, tile_height:, :tile_width],
                spread[:, tile_height:, tile_width:],
            ]
        )
        kept = lax.dynamic_slice_in_dim(quadrants, core * half, half, axis=2)
        given = lax.dynamic_slice_in_dim(quadrants, (1 - core) * half, half, axis=2)
        quadrants = kept + partner(given, 1)
        own = quadrants[0]
        from_left = from_tile(quadrants[1], 0, -1)
        from_above = from_tile(quadrants[2], -1, 0)
        from_corner = from_tile(quadrants[3], -1, -1)
        halves = z_sum(own + from_left + from_above + from_corner)
        maps = join_halves(halves, core)
        largest = tile_max(jnp.max(maps[1]))
        if batch_index + 1 < BATCHES:
            around = jnp.stack(
                [from_tile(halves, 0, 1), from_tile(halves, 1, 0), from_tile(halves, 1, 1)]
            )
            around = join_halves(around + 0.0 * largest, core)
            maps = jnp.concatenate(
                [
                    jnp.concatenate([maps, around[0]], 2),
                    jnp.concatenate([around[1], around[2]], 2),
                ],
                1,
            )
            extended = extended + 0.5 * maps[0] / (0.75 * maps[1] + 0.25 * largest)
            tile_now = extended[:tile_height, :tile_width]
        else:
            tile_now = tile_now + 0.5 * maps[0] / (0.75 * maps[1] + 0.25 * largest)
    return tile_now[None]


def solution(mesh):
    placed = (
        P("tile", None, None),
        P("wave", None, None, None),
        P("wave"),
        P("wave"),
        P("tile", None, "wave", None, None),
        P("tile", None, None),
        P("tile", None),
        P("tile", None, None),
    )
    return jax.shard_map(
        shards, mesh=mesh, in_specs=placed, out_specs=P("tile", None, None), check_vma=False
    )
```

```python
import math

import jax
import jax.numpy as jnp
from jax import lax
from jax.sharding import PartitionSpec as P

GRID_X = 8
BATCHES = 3


def tables(points):
    counter = jnp.arange(points, dtype=jnp.int32)
    angles = (
        2.0 * math.pi / points * (counter[:, None] * counter[None, :] % points).astype(jnp.float32)
    )
    factor = 1.0 / math.sqrt(points)
    return (
        (jnp.cos(angles) * factor).astype(jnp.bfloat16),
        (-jnp.sin(angles) * factor).astype(jnp.bfloat16),
    )


def left_apply(real_part, imag_part, left_real, left_imag):
    points = real_part.shape[0]
    stacked = jnp.concatenate([real_part, imag_part], 0)
    joined = jnp.concatenate([left_real, left_imag], -1)
    product = jnp.einsum("ij,...jk->...ik", stacked, joined, preferred_element_type=jnp.float32)
    return (
        product[..., :points, :points] - product[..., points:, points:],
        product[..., :points, points:] + product[..., points:, :points],
    )


def right_apply(real_part, imag_part, left_real, left_imag):
    points = real_part.shape[0]
    stacked = jnp.concatenate([real_part, imag_part], 1)
    joined = jnp.concatenate([left_real, left_imag], -2)
    product = jnp.einsum("...ij,jk->...ik", joined, stacked, preferred_element_type=jnp.float32)
    return (
        product[..., :points, :points] - product[..., points:, points:],
        product[..., :points, points:] + product[..., points:, :points],
    )


def over_waves(terms):
    total = terms[:, 0]
    for wave in range(1, terms.shape[1]):
        total = total + terms[:, wave]
    return total


def split_exact(values):
    high = lax.reduce_precision(values, exponent_bits=8, mantissa_bits=7)
    rest = values - high
    middle = lax.reduce_precision(rest, exponent_bits=8, mantissa_bits=7)
    low = rest - middle
    return jnp.stack([high, middle, low]).astype(jnp.bfloat16)


def pick(spec, picker_matrix, values, picker_first):
    parts = split_exact(values)
    ones = picker_matrix.astype(jnp.bfloat16)
    if picker_first:
        moved = jnp.einsum(spec, ones, parts, preferred_element_type=jnp.float32)
    else:
        moved = jnp.einsum(spec, parts, ones, preferred_element_type=jnp.float32)
    return (moved[0] + moved[1]) + moved[2]


def window_terms(cells, illumination, absorb, phases, measured, alive, cos_table, sin_table):
    absorb_col = absorb[None, :, None, None]
    phase_col = phases[None, :, None, None]
    spread = cells[:, None, :, :]
    magnitude = jnp.exp(-absorb_col * spread)
    object_real = magnitude * jnp.cos(phase_col * spread)
    object_imag = magnitude * jnp.sin(phase_col * spread)
    probe_real = illumination[None, :, 0]
    probe_imag = illumination[None, :, 1]
    wave_real = probe_real * object_real - probe_imag * object_imag
    wave_imag = probe_real * object_imag + probe_imag * object_real
    half_real, half_imag = left_apply(
        cos_table, sin_table, wave_real.astype(jnp.bfloat16), wave_imag.astype(jnp.bfloat16)
    )
    far_real, far_imag = right_apply(
        cos_table, sin_table, half_real.astype(jnp.bfloat16), half_imag.astype(jnp.bfloat16)
    )
    modulus = jnp.sqrt(far_real * far_real + far_imag * far_imag + 0.25)
    ratio = measured.astype(jnp.float32) / modulus
    fixed_real = (far_real * ratio).astype(jnp.bfloat16)
    fixed_imag = (far_imag * ratio).astype(jnp.bfloat16)
    back_real, back_imag = left_apply(cos_table, -sin_table, fixed_real, fixed_imag)
    new_real, new_imag = right_apply(
        cos_table, -sin_table, back_real.astype(jnp.bfloat16), back_imag.astype(jnp.bfloat16)
    )
    wave_real, wave_imag = lax.optimization_barrier((wave_real, wave_imag))
    slope_real = -absorb_col * wave_real - phase_col * wave_imag
    slope_imag = -absorb_col * wave_imag + phase_col * wave_real
    change_real = new_real - wave_real
    change_imag = new_imag - wave_imag
    weight_live = alive.astype(jnp.float32)[:, None, None]
    numerator = over_waves(slope_real * change_real + slope_imag * change_imag) * weight_live
    weights = over_waves(slope_real * slope_real + slope_imag * slope_imag) * weight_live
    return (numerator, weights)


def tile_max(value):
    count = lax.axis_size("tile")
    spread = jnp.broadcast_to(value, (count, 128))
    gathered = lax.all_to_all(spread, "tile", 0, 0, tiled=True)
    return jnp.max(gathered)


def from_tile(block, rows, columns):
    waves, tiles = lax.axis_size("wave"), lax.axis_size("tile")
    grid_rows = tiles // GRID_X
    half = GRID_X // 2
    pairs = []
    for target in range(tiles):
        row, col = target // GRID_X + rows, target % GRID_X + columns
        if not (0 <= row < grid_rows and 0 <= col < GRID_X):
            continue
        source = row * GRID_X + col
        crossing = (col // half) != ((target % GRID_X) // half)
        for wave in range(waves):
            giver = ((wave // 2 + 2) % (waves // 2)) * 2 + wave % 2 if crossing else wave
            pairs.append((giver * tiles + source, wave * tiles + target))
    return lax.ppermute(block, ("wave", "tile"), pairs)


def partner(block, bit):
    return lax.ppermute(block, "wave", [(i, i ^ bit) for i in range(lax.axis_size("wave"))])


def z_sum(block):
    bit = 2
    while bit < lax.axis_size("wave"):
        block = block + partner(block, bit)
        bit *= 2
    return block


def join_halves(block, core):
    pair = jnp.stack([block, partner(block, 1)])
    low = lax.dynamic_index_in_dim(pair, core, 0, keepdims=False)
    high = lax.dynamic_index_in_dim(pair, 1 - core, 0, keepdims=False)
    return jnp.concatenate([low, high], -2)


def picker(offsets, size, span):
    cells = lax.broadcasted_iota(jnp.int32, (offsets.shape[0], size, span), 1)
    spots = lax.broadcasted_iota(jnp.int32, (offsets.shape[0], size, span), 2)
    return (cells == spots + offsets[:, None, None]).astype(jnp.float32)


def shards(thickness, illumination, absorb, phases, amplitudes, positions, batch_order, live_slots):
    tile_now = thickness[0]
    tile_height, tile_width = tile_now.shape
    window = illumination.shape[-1]
    slots = live_slots.shape[2]
    cos_table, sin_table = tables(window)
    core = lax.axis_index("wave") % 2
    half = tile_height // 2
    rows = lax.dynamic_slice_in_dim(tile_now, core * half, half, axis=0)
    halo = jnp.stack([from_tile(rows, 0, 1), from_tile(rows, 1, 0), from_tile(rows, 1, 1)])
    right, below, corner = join_halves(halo, core)
    extended = jnp.concatenate(
        [jnp.concatenate([tile_now, right], 1), jnp.concatenate([below, corner], 1)], 0
    )
    for batch_index in range(BATCHES):
        chosen = batch_order[0, batch_index * slots : (batch_index + 1) * slots]
        places = positions[0][chosen]
        measured = amplitudes[0][chosen]
        alive = live_slots[0, batch_index]
        row_pick = picker(places[:, 0], tile_height + window, window)
        col_pick = picker(places[:, 1], tile_width + window, window)
        strips = pick("sij,pik->psjk", row_pick, extended, True)
        cells = pick("psjk,skl->psjl", col_pick, strips, False)
        numer_win, weight_win = window_terms(
            cells, illumination, absorb, phases, measured, alive, cos_table, sin_table
        )
        wins = jnp.stack([numer_win, weight_win], 1)
        placed_rows = pick("sij,psmjk->psmik", row_pick, wins, True)
        spread = pick("psmik,slk->pmil", col_pick, placed_rows, False)
        quadrants = jnp.stack(
            [
                spread[:, :tile_height, :tile_width],
                spread[:, :tile_height, tile_width:],
                spread[:, tile_height:, :tile_width],
                spread[:, tile_height:, tile_width:],
            ]
        )
        kept = lax.dynamic_slice_in_dim(quadrants, core * half, half, axis=2)
        given = lax.dynamic_slice_in_dim(quadrants, (1 - core) * half, half, axis=2)
        quadrants = kept + partner(given, 1)
        own = quadrants[0]
        from_left = from_tile(quadrants[1], 0, -1)
        from_above = from_tile(quadrants[2], -1, 0)
        from_corner = from_tile(quadrants[3], -1, -1)
        halves = z_sum(own + from_left + from_above + from_corner)
        maps = join_halves(halves, core)
        largest = tile_max(jnp.max(maps[1]))
        if batch_index + 1 < BATCHES:
            around = jnp.stack(
                [from_tile(halves, 0, 1), from_tile(halves, 1, 0), from_tile(halves, 1, 1)]
            )
            around = join_halves(around + 0.0 * largest, core)
            maps = jnp.concatenate(
                [
                    jnp.concatenate([maps, around[0]], 2),
                    jnp.concatenate([around[1], around[2]], 2),
                ],
                1,
            )
            extended = extended + 0.5 * maps[0] / (0.75 * maps[1] + 0.25 * largest)
            tile_now = extended[:tile_height, :tile_width]
        else:
            tile_now = tile_now + 0.5 * maps[0] / (0.75 * maps[1] + 0.25 * largest)
    return tile_now[None]


def solution(mesh):
    placed = (
        P("tile", None, None),
        P("wave", None, None, None),
        P("wave"),
        P("wave"),
        P("tile", None, "wave", None, None),
        P("tile", None, None),
        P("tile", None),
        P("tile", None, None),
    )
    return jax.shard_map(
        shards, mesh=mesh, in_specs=placed, out_specs=P("tile", None, None), check_vma=False
    )
```

```python
import math

import jax
import jax.numpy as jnp
from jax import lax
from jax.sharding import PartitionSpec as P

GRID_X = 8
BATCHES = 3


def tables(points):
    counter = jnp.arange(points, dtype=jnp.int32)
    angles = (
        2.0 * math.pi / points * (counter[:, None] * counter[None, :] % points).astype(jnp.float32)
    )
    factor = 1.0 / math.sqrt(points)
    return (
        (jnp.cos(angles) * factor).astype(jnp.bfloat16),
        (-jnp.sin(angles) * factor).astype(jnp.bfloat16),
    )


def left_apply(real_part, imag_part, left_real, left_imag):
    points = real_part.shape[0]
    stacked = jnp.concatenate([real_part, imag_part], 0)
    joined = jnp.concatenate([left_real, left_imag], -1)
    product = jnp.einsum("ij,...jk->...ik", stacked, joined, preferred_element_type=jnp.float32)
    return (
        product[..., :points, :points] - product[..., points:, points:],
        product[..., :points, points:] + product[..., points:, :points],
    )


def right_apply(real_part, imag_part, left_real, left_imag):
    points = real_part.shape[0]
    stacked = jnp.concatenate([real_part, imag_part], 1)
    joined = jnp.concatenate([left_real, left_imag], -2)
    product = jnp.einsum("...ij,jk->...ik", joined, stacked, preferred_element_type=jnp.float32)
    return (
        product[..., :points, :points] - product[..., points:, points:],
        product[..., :points, points:] + product[..., points:, :points],
    )


def over_waves(terms):
    total = terms[:, 0]
    for wave in range(1, terms.shape[1]):
        total = total + terms[:, wave]
    return total


def split_exact(values):
    high = lax.reduce_precision(values, exponent_bits=8, mantissa_bits=7)
    rest = values - high
    middle = lax.reduce_precision(rest, exponent_bits=8, mantissa_bits=7)
    low = rest - middle
    return jnp.stack([high, middle, low]).astype(jnp.bfloat16)


def pick(spec, picker_matrix, values, picker_first):
    parts = split_exact(values)
    ones = picker_matrix.astype(jnp.bfloat16)
    if picker_first:
        moved = jnp.einsum(spec, ones, parts, preferred_element_type=jnp.float32)
    else:
        moved = jnp.einsum(spec, parts, ones, preferred_element_type=jnp.float32)
    return (moved[0] + moved[1]) + moved[2]


def window_terms(cells, illumination, absorb, phases, measured, alive, cos_table, sin_table):
    absorb_col = absorb[None, :, None, None]
    phase_col = phases[None, :, None, None]
    spread = cells[:, None, :, :]
    magnitude = jnp.exp(-absorb_col * spread)
    object_real = magnitude * jnp.cos(phase_col * spread)
    object_imag = magnitude * jnp.sin(phase_col * spread)
    probe_real = illumination[None, :, 0]
    probe_imag = illumination[None, :, 1]
    wave_real = probe_real * object_real - probe_imag * object_imag
    wave_imag = probe_real * object_imag + probe_imag * object_real
    half_real, half_imag = left_apply(
        cos_table, sin_table, wave_real.astype(jnp.bfloat16), wave_imag.astype(jnp.bfloat16)
    )
    far_real, far_imag = right_apply(
        cos_table, sin_table, half_real.astype(jnp.bfloat16), half_imag.astype(jnp.bfloat16)
    )
    modulus = jnp.sqrt(far_real * far_real + far_imag * far_imag + 0.25)
    ratio = measured.astype(jnp.float32) / modulus
    fixed_real = (far_real * ratio).astype(jnp.bfloat16)
    fixed_imag = (far_imag * ratio).astype(jnp.bfloat16)
    back_real, back_imag = left_apply(cos_table, -sin_table, fixed_real, fixed_imag)
    new_real, new_imag = right_apply(
        cos_table, -sin_table, back_real.astype(jnp.bfloat16), back_imag.astype(jnp.bfloat16)
    )
    wave_real, wave_imag = lax.optimization_barrier((wave_real, wave_imag))
    slope_real = -absorb_col * wave_real - phase_col * wave_imag
    slope_imag = -absorb_col * wave_imag + phase_col * wave_real
    change_real = new_real - wave_real
    change_imag = new_imag - wave_imag
    weight_live = alive.astype(jnp.float32)[:, None, None]
    numerator = over_waves(slope_real * change_real + slope_imag * change_imag) * weight_live
    weights = over_waves(slope_real * slope_real + slope_imag * slope_imag) * weight_live
    return (numerator, weights)


def tile_max(value):
    count = lax.axis_size("tile")
    spread = jnp.broadcast_to(value, (count, 128))
    gathered = lax.all_to_all(spread, "tile", 0, 0, tiled=True)
    return jnp.max(gathered)


def from_tile(block, rows, columns):
    waves, tiles = lax.axis_size("wave"), lax.axis_size("tile")
    grid_rows = tiles // GRID_X
    half = GRID_X // 2
    pairs = []
    for target in range(tiles):
        row, col = target // GRID_X + rows, target % GRID_X + columns
        if not (0 <= row < grid_rows and 0 <= col < GRID_X):
            continue
        source = row * GRID_X + col
        crossing = (col // half) != ((target % GRID_X) // half)
        for wave in range(waves):
            giver = ((wave // 2 + 2) % (waves // 2)) * 2 + wave % 2 if crossing else wave
            pairs.append((giver * tiles + source, wave * tiles + target))
    return lax.ppermute(block, ("wave", "tile"), pairs)


def partner(block, bit):
    return lax.ppermute(block, "wave", [(i, i ^ bit) for i in range(lax.axis_size("wave"))])


def z_sum(block):
    bit = lax.axis_size("wave") // 2
    while bit >= 2:
        block = block + partner(block, bit)
        bit //= 2
    return block


def join_halves(block, core):
    other = partner(block, 1)
    low = jnp.where(core == 0, block, other)
    high = jnp.where(core == 0, other, block)
    return jnp.concatenate([low, high], -2)


def picker(offsets, size, span):
    cells = lax.broadcasted_iota(jnp.int32, (offsets.shape[0], size, span), 1)
    spots = lax.broadcasted_iota(jnp.int32, (offsets.shape[0], size, span), 2)
    return (cells == spots + offsets[:, None, None]).astype(jnp.float32)


def shards(thickness, illumination, absorb, phases, amplitudes, positions, batch_order, live_slots):
    tile_now = thickness[0]
    tile_height, tile_width = tile_now.shape
    window = illumination.shape[-1]
    slots = live_slots.shape[2]
    cos_table, sin_table = tables(window)
    core = lax.axis_index("wave") % 2
    half = tile_height // 2
    rows = lax.dynamic_slice_in_dim(tile_now, core * half, half, axis=0)
    halo = jnp.stack([from_tile(rows, 0, 1), from_tile(rows, 1, 0), from_tile(rows, 1, 1)])
    right, below, corner = join_halves(halo, core)
    extended = jnp.concatenate(
        [jnp.concatenate([tile_now, right], 1), jnp.concatenate([below, corner], 1)], 0
    )
    for batch_index in range(BATCHES):
        chosen = batch_order[0, batch_index * slots : (batch_index + 1) * slots]
        places = positions[0][chosen]
        measured = amplitudes[0][chosen]
        alive = live_slots[0, batch_index]
        row_pick = picker(places[:, 0], tile_height + window, window)
        col_pick = picker(places[:, 1], tile_width + window, window)
        strips = pick("sij,pik->psjk", row_pick, extended, True)
        cells = pick("psjk,skl->psjl", col_pick, strips, False)
        numer_win, weight_win = window_terms(
            cells, illumination, absorb, phases, measured, alive, cos_table, sin_table
        )
        wins = jnp.stack([numer_win, weight_win], 1)
        placed_rows = pick("sij,psmjk->psmik", row_pick, wins, True)
        spread = pick("psmik,slk->pmil", col_pick, placed_rows, False)
        quadrants = jnp.stack(
            [
                spread[:, :tile_height, :tile_width],
                spread[:, :tile_height, tile_width:],
                spread[:, tile_height:, :tile_width],
                spread[:, tile_height:, tile_width:],
            ]
        )
        kept = lax.dynamic_slice_in_dim(quadrants, core * half, half, axis=2)
        given = lax.dynamic_slice_in_dim(quadrants, (1 - core) * half, half, axis=2)
        quadrants = kept + partner(given, 1)
        own = quadrants[0]
        from_left = from_tile(quadrants[1], 0, -1)
        from_above = from_tile(quadrants[2], -1, 0)
        from_corner = from_tile(quadrants[3], -1, -1)
        halves = z_sum(own + from_left + from_above + from_corner)
        maps = join_halves(halves, core)
        largest = tile_max(jnp.max(maps[1]))
        if batch_index + 1 < BATCHES:
            around = jnp.stack(
                [from_tile(halves, 0, 1), from_tile(halves, 1, 0), from_tile(halves, 1, 1)]
            )
            around = join_halves(around + 0.0 * largest, core)
            maps = jnp.concatenate(
                [
                    jnp.concatenate([maps, around[0]], 2),
                    jnp.concatenate([around[1], around[2]], 2),
                ],
                1,
            )
            extended = extended + 0.5 * maps[0] / (0.75 * maps[1] + 0.25 * largest)
            tile_now = extended[:tile_height, :tile_width]
        else:
            tile_now = tile_now + 0.5 * maps[0] / (0.75 * maps[1] + 0.25 * largest)
    return tile_now[None]


def solution(mesh):
    placed = (
        P("tile", None, None),
        P("wave", None, None, None),
        P("wave"),
        P("wave"),
        P("tile", None, "wave", None, None),
        P("tile", None, None),
        P("tile", None),
        P("tile", None, None),
    )
    return jax.shard_map(
        shards, mesh=mesh, in_specs=placed, out_specs=P("tile", None, None), check_vma=False
    )
```
